32 devices in a mesh: group: 4 (over z), member: 8 (over y, x, core).
Axes of the slice: x: 2, y: 2, z: 4, core: 2. Of those that a mesh axis runs over, the one named last changes fastest.
Arguments:
- tile_values: bfloat16 [128, 512, 512], P(('group', 'member')), may hold values from -0.0625 to 0.0625
- tile_lists: int32 [128, 3], P(('group', 'member')), may hold values from 0 to 7, as said below
- owner_map: int32 [4, 8], P('group'), may hold values from 0 to 7, as said below
- inverses: bfloat16 [32, 512, 512], P(('group', 'member')), as said below
- excitations: float32 [3, 32, 32, 512], P(None, ('group', 'member')), may hold values from -6 to 6
- history: bfloat16 [2, 32, 32, 512], P(None, ('group', 'member')), may hold values from -6 to 6
Outputs:
- currents: float32 [3, 32, 32, 512], P(None, ('group', 'member'))
The draws below stay inside these ranges and needn't reach their ends.
Inputs may be any that keep to these rules, and one draw needn't show every extreme that they name: `owner_map`: each row is a permutation of the members. `tile_lists`: rows d * 4 to d * 4 + 3 belong to device d = g * 8 + m. Delay tag 0 marks an empty slot; a live tile has a delay tag of 1 to 2, an observer block of its own group (g * 2 to g * 2 + 1), and the live tiles of one device take their source blocks from different groups (source block // 2). Every device has 2 or more live tiles; in every group some device has 4. `inverses`: the 4 owners of one block hold the same matrix.
All inputs are finite; a program needn't handle non-finite values.
Results may differ from the reference program's by a relative error of at most 0.025.
Values may be sent and summed in bfloat16 or wider, within the bound.
No kernel may reach another device: no remote copies, remote signals or barrier semaphores. Data moves between devices by JAX's collectives and lax.ppermute only.
A program may use at most 64 MiB of HBM per device.

```python
import math
import jax
import jax.numpy as jnp
from jax import lax

BLOCK = 512
EXCITE = 128
OWNERS = 4
SHARE = 32
GROUP_BLOCKS = 2
BLOCKS = 8
TILES = 4
DELAYS = 2
STEPS = 3
N_GROUP = 4
N_MEMBER = 8


def owner_table(key):
    keys = jax.random.split(jax.random.fold_in(key, 7), N_GROUP)
    return jax.vmap(lambda single: jax.random.permutation(single, N_MEMBER))(keys).astype(jnp.int32)


def draw_owner_map(key, part):
    return owner_table(key)


def draw_inverses(key, part):
    owners = owner_table(key)
    member_ids = jnp.arange(N_MEMBER, dtype=jnp.int32)
    matches = owners[:, :, None] == member_ids[None, None, :]
    slot_of = jnp.sum(jnp.where(matches, member_ids[None, :, None], 0), axis=1)
    group_ids = jnp.arange(N_GROUP, dtype=jnp.int32)
    block_of = (group_ids[:, None] * GROUP_BLOCKS + slot_of // OWNERS).reshape(-1)
    base_key = jax.random.fold_in(key, 11)

    def one_block(block):
        block_key = jax.random.fold_in(base_key, block)
        key_diag, key_noise = jax.random.split(block_key)
        diagonal = jnp.exp(jax.random.uniform(key_diag, (BLOCK,), jnp.float32, math.log(0.5), math.log(2.0)))
        noise = jax.random.normal(key_noise, (BLOCK, BLOCK), jnp.float32) * (0.5 / math.sqrt(BLOCK))
        eye = jnp.eye(BLOCK, dtype=jnp.float32)
        return (eye * diagonal[:, None] + noise).astype(jnp.bfloat16)
    return jax.lax.map(one_block, block_of)


def draw_tile_lists(key, part):
    devices = N_GROUP * N_MEMBER
    keys = jax.random.split(jax.random.fold_in(key, 3), 7)
    active_count = jax.random.randint(keys[0], (devices,), 2, TILES + 1)
    full_member = jax.random.randint(keys[1], (N_GROUP,), 0, N_MEMBER)
    is_full = (jnp.arange(N_MEMBER)[None, :] == full_member[:, None]).reshape(devices)
    active_count = jnp.where(is_full, TILES, active_count)
    source_groups = jax.vmap(lambda single: jax.random.permutation(single, N_GROUP)[:TILES])(jax.random.split(keys[2], devices))
    positions = jax.vmap(lambda single: jax.random.permutation(single, TILES))(jax.random.split(keys[3], devices))
    source_local = jax.random.randint(keys[4], (devices, TILES), 0, GROUP_BLOCKS)
    observer_local = jax.random.randint(keys[5], (devices, TILES), 0, GROUP_BLOCKS)
    slot_ids = jnp.arange(TILES)[None, :]
    observer_local = jnp.where(is_full[:, None] & (slot_ids == 0), GROUP_BLOCKS - 1, observer_local)
    observer_local = jnp.where(is_full[:, None] & (slot_ids == 1), 0, observer_local)
    delay_tags = jax.random.randint(keys[6], (devices, TILES), 1, DELAYS + 1)
    delay_tags = jnp.where(positions < active_count[:, None], delay_tags, 0)
    home_group = jnp.arange(devices) // N_MEMBER
    source = source_groups * GROUP_BLOCKS + source_local
    observer = home_group[:, None] * GROUP_BLOCKS + observer_local
    table = jnp.stack([source, observer, delay_tags], axis=-1)
    return table.reshape(devices * TILES, 3).astype(jnp.int32)


def levels(key, dims, cuts, smallest, largest):
    level = 1.0
    for position, parts in cuts:
        draws = jax.random.uniform(jax.random.fold_in(jax.random.fold_in(key, 6), position), (parts,), jnp.float32, smallest / len(cuts), largest / len(cuts))
        level = level * jnp.repeat(jnp.exp(draws), dims[position] // parts).reshape((-1,) + (1,) * (len(dims) - 1 - position))
    return level


def scatter_about(stream_key, shape, scale, bound, cuts=(), kind=jnp.bfloat16):
    loudness = levels(stream_key, shape, cuts, -0.22, 0.18) if cuts else 1.0
    result = jax.random.normal(stream_key, shape, jnp.float32) * scale * loudness
    return jnp.minimum(jnp.maximum(result, -bound), bound).astype(kind)


def setup_inputs(seed: int = 0) -> dict:
    key_list = jax.random.split(jax.random.key(seed), 7)
    tile_values = scatter_about(key_list[0], (N_GROUP * N_MEMBER * TILES, BLOCK, BLOCK), (16 * BLOCK) ** -0.5, 0.0625, ((0, 32),))
    tile_lists = draw_tile_lists(jax.random.fold_in(key_list[6], 71), 0)
    owner_map = draw_owner_map(jax.random.fold_in(key_list[6], 71), 0)
    inverses = draw_inverses(jax.random.fold_in(key_list[6], 71), 0)
    excitations = scatter_about(key_list[4], (STEPS, N_GROUP * N_MEMBER, SHARE, BLOCK), 1.0, 6.0, ((1, 32),), jnp.float32)
    history = scatter_about(key_list[5], (DELAYS, N_GROUP * N_MEMBER, SHARE, BLOCK), 1.0, 6.0, ((1, 32),))
    return {"tile_values": tile_values, "tile_lists": tile_lists, "owner_map": owner_map, "inverses": inverses, "excitations": excitations, "history": history}


def member_slots(owner_map):
    member_ids = jnp.arange(N_MEMBER, dtype=jnp.int32)
    matches = owner_map[:, :, None] == member_ids[None, None, :]
    return jnp.sum(jnp.where(matches, member_ids[None, :, None], 0), axis=1).astype(jnp.int32)


def to_blocks(pieces, owner_map):
    grouped = pieces.reshape(N_GROUP, N_MEMBER, SHARE, BLOCK)
    ordered = jax.vmap(lambda rows_in, owner_row: jnp.take(rows_in, owner_row, axis=0))(grouped, owner_map)
    return ordered.reshape(BLOCKS, EXCITE, BLOCK)


def to_owners(field, owner_map):
    slots = field.reshape(N_GROUP, N_MEMBER, SHARE, BLOCK)
    slot_of = member_slots(owner_map)
    return jax.vmap(lambda rows_in, order: jnp.take(rows_in, order, axis=0))(slots, slot_of)


def reference(tile_values, tile_lists, owner_map, inverses, excitations, history):
    timeline = jnp.zeros((DELAYS + STEPS, BLOCKS, EXCITE, BLOCK), jnp.bfloat16)
    for index in range(DELAYS):
        timeline = timeline.at[index].set(to_blocks(history[index], owner_map))
    lists = tile_lists.reshape(N_GROUP, N_MEMBER * TILES, 3)
    values = tile_values.reshape(N_GROUP, N_MEMBER * TILES, BLOCK, BLOCK)
    inverse_f = inverses.astype(jnp.float32).reshape(N_GROUP, N_MEMBER, BLOCK, BLOCK)
    block_ids = jnp.arange(GROUP_BLOCKS, dtype=jnp.int32)
    outputs = []
    for step in range(STEPS):
        def group_field(carry, packed):
            entries, matrices, group_index = packed
            source = entries[:, 0]
            observer = entries[:, 1]
            delays_here = entries[:, 2]
            when = (DELAYS + step - delays_here).astype(jnp.int32)
            inputs = timeline[when, source]
            products_f = jnp.einsum("kes,kso->keo", inputs.astype(jnp.float32), matrices.astype(jnp.float32),
                                    precision=lax.Precision.HIGHEST)
            local_obs = observer - group_index * GROUP_BLOCKS
            one_hot = ((local_obs[:, None] == block_ids[None, :]) & (delays_here[:, None] > 0)).astype(jnp.float32)
            one_hot = one_hot.reshape(N_MEMBER, TILES, GROUP_BLOCKS)
            partial_value = jnp.einsum("mtb,mteo->mbeo", one_hot, products_f.reshape(N_MEMBER, TILES, EXCITE, BLOCK),
                                 precision=lax.Precision.HIGHEST)
            rounded = lax.optimization_barrier(partial_value.astype(jnp.bfloat16))
            return carry, jnp.sum(rounded.astype(jnp.float32), axis=0)

        _, fields = lax.scan(group_field, jnp.zeros((), jnp.float32),
                             (lists, values, jnp.arange(N_GROUP, dtype=jnp.int32)))
        field_own = to_owners(fields.reshape(BLOCKS, EXCITE, BLOCK), owner_map)
        residual = (excitations[step].reshape(N_GROUP, N_MEMBER, SHARE, BLOCK) - field_own).astype(jnp.bfloat16)
        residual = lax.optimization_barrier(residual)
        currents = jnp.einsum("gmsi,gmij->gmsj", residual.astype(jnp.float32), inverse_f,
                              precision=lax.Precision.HIGHEST)
        outputs.append(currents.reshape(N_GROUP * N_MEMBER, SHARE, BLOCK))
        timeline = timeline.at[DELAYS + step].set(
            to_blocks(currents.astype(jnp.bfloat16).reshape(N_GROUP * N_MEMBER, SHARE, BLOCK), owner_map))
    return jnp.stack(outputs)
```

```python
import jax
import jax.numpy as jnp
from jax import lax
from jax.sharding import PartitionSpec as P

BLOCK = 512
EXCITE = 128
OWNERS = 4
DELAYS = 2
STEPS = 3


def shift_gather(x, axis, n):
    pieces = [x]
    for k in range(1, n):
        pieces.append(lax.ppermute(x, axis, [(i, (i + k) % n) for i in range(n)]))
    return jnp.stack(pieces)


def shift_exchange(x, axis, n, here):
    pieces = [lax.dynamic_index_in_dim(x, here, 0, keepdims=False)]
    for k in range(1, n):
        piece = lax.dynamic_index_in_dim(x, (here + k) % n, 0, keepdims=False)
        pieces.append(lax.ppermute(piece, axis, [(i, (i + k) % n) for i in range(n)]))
    return jnp.stack(pieces)


def select_rows(timeline, peer_lists, times_wanted, wanted, group_here, group_blocks, last_time):
    source = peer_lists[:, :, 0]
    from_here = source // group_blocks == group_here
    chosen_mask = wanted & from_here
    clipped = jnp.clip(times_wanted, 0, last_time)
    flat_index = clipped * group_blocks + source % group_blocks
    picked = jnp.sum(jnp.where(chosen_mask, flat_index, 0), axis=1)
    filled = jnp.any(chosen_mask, axis=1)
    picked_rows = jnp.take(timeline, picked, axis=0)
    return jnp.where(filled[:, None, None], picked_rows, jnp.zeros_like(picked_rows))


def body(tile_values, tile_lists, owner_map, inverses, excitations, history):
    members = lax.axis_size("member")
    groups = lax.axis_size("group")
    group_blocks = members // OWNERS
    share = EXCITE // OWNERS
    group_here = lax.axis_index("group")
    member_here = lax.axis_index("member")
    tiles_here = tile_lists.shape[0]
    last_time = DELAYS + STEPS - 1
    owners = owner_map[0]
    member_ids = jnp.arange(members, dtype=jnp.int32)
    matches = owners[:, None] == member_ids[None, :]
    slot_of_member = jnp.sum(jnp.where(matches, member_ids[:, None], 0), axis=0)
    by_shift = shift_gather(tile_lists, "group", groups)
    peer_lists = jnp.take(by_shift, (group_here - jnp.arange(groups)) % groups, axis=0)
    peer_delays = peer_lists[:, :, 2]
    peer_active = peer_delays > 0
    owner_shift = (member_here - owners) % members
    gathered = shift_gather(history[:, 0], "member", members)
    ordered = jnp.take(gathered, owner_shift, axis=0)
    ordered = jnp.moveaxis(ordered, 1, 0).reshape(DELAYS * group_blocks, EXCITE, BLOCK)
    timeline = jnp.concatenate(
        [ordered, jnp.zeros((STEPS * group_blocks, EXCITE, BLOCK), jnp.bfloat16)], axis=0
    )
    source_group = tile_lists[:, 0] // group_blocks
    observer_local = tile_lists[:, 1] % group_blocks
    delays_here = tile_lists[:, 2]
    source_shift = (group_here - source_group) % groups
    results = []
    for step in range(STEPS):
        outgoing = select_rows(
            timeline,
            peer_lists,
            DELAYS + step - peer_delays,
            peer_active,
            group_here,
            group_blocks,
            last_time,
        )
        incoming = shift_exchange(outgoing, "group", groups, group_here)
        blocks_in = jnp.take(incoming, source_shift, axis=0)
        terms = jnp.einsum(
            "kes,kso->keo", blocks_in, tile_values, preferred_element_type=jnp.float32
        )
        partial_sums = []
        for block in range(group_blocks):
            chosen = (observer_local == block) & (delays_here > 0)
            partial_sums.append(
                jnp.sum(jnp.where(chosen[:, None, None], terms, 0.0), axis=0)
            )
        slots = jnp.stack(partial_sums).astype(jnp.bfloat16).reshape(members, share, BLOCK)
        sent = jnp.take(slots, slot_of_member, axis=0)
        pieces = shift_exchange(sent, "member", members, member_here)
        field = jnp.sum(pieces.astype(jnp.float32), axis=0)
        residual = (excitations[step, 0] - field).astype(jnp.bfloat16)
        current = jnp.dot(residual, inverses[0], preferred_element_type=jnp.float32)
        results.append(current)
        if step + 1 < STEPS:
            whole = shift_gather(current.astype(jnp.bfloat16), "member", members)
            placed = jnp.take(whole, owner_shift, axis=0).reshape(group_blocks, EXCITE, BLOCK)
            timeline = lax.dynamic_update_slice_in_dim(
                timeline, placed, (DELAYS + step) * group_blocks, 0
            )
    return jnp.stack(results)[:, None]


def solution(mesh):
    placed = (
        P(("group", "member"), None, None),
        P(("group", "member"), None),
        P("group", None),
        P(("group", "member"), None, None),
        P(None, ("group", "member"), None, None),
        P(None, ("group", "member"), None, None),
    )
    return jax.shard_map(
        body,
        mesh=mesh,
        in_specs=placed,
        out_specs=P(None, ("group", "member"), None, None),
        check_vma=False,
    )
```

```python
import jax
import jax.numpy as jnp
from jax import lax
from jax.sharding import PartitionSpec as P

BLOCK = 512
EXCITE = 128
OWNERS = 4
DELAYS = 2
STEPS = 3


def shifted(x, axis, n, k):
    return lax.ppermute(x, axis, [(i, (i + k) % n) for i in range(n)])


def shift_gather(x, axis, n):
    return [x] + [shifted(x, axis, n, k) for k in range(1, n)]


def pick(pieces, index):
    if len(pieces) <= 8:
        return jnp.stack([lax.select_n(index[i], *pieces) for i in range(index.shape[0])])
    return jnp.take(jnp.stack(pieces), index, axis=0)


def body(tile_values, tile_lists, owner_map, inverses, excitations, history):
    members = lax.axis_size("member")
    groups = lax.axis_size("group")
    group_blocks = members // OWNERS
    share = EXCITE // OWNERS
    group_here = lax.axis_index("group")
    member_here = lax.axis_index("member")
    owners = owner_map[0]
    member_ids = jnp.arange(members, dtype=jnp.int32)
    matches = owners[:, None] == member_ids[None, :]
    slot_of_member = jnp.sum(jnp.where(matches, member_ids[:, None], 0), axis=0)
    owner_shift = (member_here - owners) % members
    send_slot = jnp.take(slot_of_member, (member_here + member_ids) % members)

    lists_by_shift = jnp.stack(shift_gather(tile_lists, "group", groups))
    group_ids = jnp.arange(groups, dtype=jnp.int32)
    ahead = jnp.take(lists_by_shift, (groups - group_ids) % groups, axis=0)
    wanted = (ahead[:, :, 0] // group_blocks == group_here) & (ahead[:, :, 2] > 0)
    want_block = jnp.sum(jnp.where(wanted, ahead[:, :, 0] % group_blocks, 0), axis=1)
    want_delay = jnp.sum(jnp.where(wanted, ahead[:, :, 2], 0), axis=1)

    source_group = tile_lists[:, 0] // group_blocks
    observer_local = tile_lists[:, 1] % group_blocks
    delays_here = tile_lists[:, 2]
    source_shift = (group_here - source_group) % groups

    hist_pieces = shift_gather(history[:, 0], "member", members)
    hist_placed = pick(hist_pieces, owner_shift)
    blocks = [
        hist_placed[:, t].reshape(group_blocks, EXCITE, BLOCK) for t in range(DELAYS)
    ]
    results = []
    for step in range(STEPS):
        near = blocks[DELAYS + step - 1]
        far = blocks[DELAYS + step - 2]
        received = []
        for k in range(groups):
            a = lax.dynamic_index_in_dim(near, want_block[k], 0, keepdims=False)
            b = lax.dynamic_index_in_dim(far, want_block[k], 0, keepdims=False)
            piece = jnp.where(
                want_delay[k] == 1, a, jnp.where(want_delay[k] == 2, b, jnp.zeros_like(a))
            )
            received.append(piece if k == 0 else shifted(piece, "group", groups, k))
        blocks_in = pick(received, source_shift)
        terms = jnp.einsum(
            "kes,kso->keo", blocks_in, tile_values, preferred_element_type=jnp.float32
        )
        partial_sums = []
        for block in range(group_blocks):
            chosen = (observer_local == block) & (delays_here > 0)
            partial_sums.append(
                jnp.sum(jnp.where(chosen[:, None, None], terms, 0.0), axis=0)
            )
        slots = jnp.stack(partial_sums).astype(jnp.bfloat16).reshape(members, share, BLOCK)
        field = slots[0].astype(jnp.float32) * 0.0
        for k in range(members):
            piece = lax.dynamic_index_in_dim(slots, send_slot[k], 0, keepdims=False)
            if k:
                piece = shifted(piece, "member", members, k)
            field = field + piece.astype(jnp.float32)
        residual = (excitations[step, 0] - field).astype(jnp.bfloat16)
        current = jnp.dot(residual, inverses[0], preferred_element_type=jnp.float32)
        results.append(current)
        if step + 1 < STEPS:
            pieces = shift_gather(current.astype(jnp.bfloat16), "member", members)
            blocks.append(pick(pieces, owner_shift).reshape(group_blocks, EXCITE, BLOCK))
    return jnp.stack(results)[:, None]


def solution(mesh):
    placed = (
        P(("group", "member"), None, None),
        P(("group", "member"), None),
        P("group", None),
        P(("group", "member"), None, None),
        P(None, ("group", "member"), None, None),
        P(None, ("group", "member"), None, None),
    )
    return jax.shard_map(
        body,
        mesh=mesh,
        in_specs=placed,
        out_specs=P(None, ("group", "member"), None, None),
        check_vma=False,
    )
```

```python
import jax
import jax.numpy as jnp
from jax import lax
from jax.sharding import PartitionSpec as P

BLOCK = 512
EXCITE = 128
OWNERS = 4
DELAYS = 2
STEPS = 3


def shifted(x, axis, n, k):
    return lax.ppermute(x, axis, [(i, (i + k) % n) for i in range(n)])


def shift_gather(x, axis, n):
    return [x] + [shifted(x, axis, n, k) for k in range(1, n)]


def pick(pieces, index):
    if len(pieces) > 8:
        return jnp.take(jnp.stack(pieces), index, axis=0)
    chosen = index[:, None] == jnp.arange(len(pieces), dtype=index.dtype)[None, :]
    spread = (slice(None),) + (None,) * pieces[0].ndim
    total = None
    for k, piece in enumerate(pieces):
        term = jnp.where(chosen[:, k][spread], piece[None], jnp.zeros_like(piece)[None])
        total = term if total is None else total + term
    return total


def body(tile_values, tile_lists, owner_map, inverses, excitations, history):
    members = lax.axis_size("member")
    groups = lax.axis_size("group")
    group_blocks = members // OWNERS
    share = EXCITE // OWNERS
    group_here = lax.axis_index("group")
    member_here = lax.axis_index("member")
    owners = owner_map[0]
    member_ids = jnp.arange(members, dtype=jnp.int32)
    matches = owners[:, None] == member_ids[None, :]
    slot_of_member = jnp.sum(jnp.where(matches, member_ids[:, None], 0), axis=0)
    owner_shift = (member_here - owners) % members
    send_slot = jnp.take(slot_of_member, (member_here + member_ids) % members)

    lists_by_shift = jnp.stack(shift_gather(tile_lists, "group", groups))
    group_ids = jnp.arange(groups, dtype=jnp.int32)
    ahead = jnp.take(lists_by_shift, (groups - group_ids) % groups, axis=0)
    wanted = (ahead[:, :, 0] // group_blocks == group_here) & (ahead[:, :, 2] > 0)
    want_block = jnp.sum(jnp.where(wanted, ahead[:, :, 0] % group_blocks, 0), axis=1)
    want_delay = jnp.sum(jnp.where(wanted, ahead[:, :, 2], 0), axis=1)
    block_ids = jnp.arange(group_blocks, dtype=jnp.int32)
    which_block = want_block[:, None] == block_ids[None, :]
    from_near = which_block & (want_delay[:, None] == 1)
    from_far = which_block & (want_delay[:, None] == 2)

    source_group = tile_lists[:, 0] // group_blocks
    observer_local = tile_lists[:, 1] % group_blocks
    delays_here = tile_lists[:, 2]
    source_shift = (group_here - source_group) % groups

    hist_pieces = shift_gather(history[:, 0], "member", members)
    hist_placed = pick(hist_pieces, owner_shift)
    blocks = [
        hist_placed[:, t].reshape(group_blocks, EXCITE, BLOCK) for t in range(DELAYS)
    ]
    results = []
    for step in range(STEPS):
        near = blocks[DELAYS + step - 1]
        far = blocks[DELAYS + step - 2]
        outgoing = None
        for block in range(group_blocks):
            term = jnp.where(from_near[:, block, None, None], near[block][None], 0) + jnp.where(
                from_far[:, block, None, None], far[block][None], 0
            )
            outgoing = term if outgoing is None else outgoing + term
        received = [outgoing[0]] + [
            shifted(outgoing[k], "group", groups, k) for k in range(1, groups)
        ]
        blocks_in = pick(received, source_shift)
        terms = jnp.einsum(
            "kes,kso->keo", blocks_in, tile_values, preferred_element_type=jnp.float32
        )
        partial_sums = []
        for block in range(group_blocks):
            chosen = (observer_local == block) & (delays_here > 0)
            partial_sums.append(
                jnp.sum(jnp.where(chosen[:, None, None], terms, 0.0), axis=0)
            )
        slots = jnp.stack(partial_sums).astype(jnp.bfloat16).reshape(members, share, BLOCK)
        field = slots[0].astype(jnp.float32) * 0.0
        for k in range(members):
            piece = lax.dynamic_index_in_dim(slots, send_slot[k], 0, keepdims=False)
            if k:
                piece = shifted(piece, "member", members, k)
            field = field + piece.astype(jnp.float32)
        residual = (excitations[step, 0] - field).astype(jnp.bfloat16)
        current = jnp.dot(residual, inverses[0], preferred_element_type=jnp.float32)
        results.append(current)
        if step + 1 < STEPS:
            pieces = shift_gather(current.astype(jnp.bfloat16), "member", members)
            blocks.append(pick(pieces, owner_shift).reshape(group_blocks, EXCITE, BLOCK))
    return jnp.stack(results)[:, None]


def solution(mesh):
    placed = (
        P(("group", "member"), None, None),
        P(("group", "member"), None),
        P("group", None),
        P(("group", "member"), None, None),
        P(None, ("group", "member"), None, None),
        P(None, ("group", "member"), None, None),
    )
    return jax.shard_map(
        body,
        mesh=mesh,
        in_specs=placed,
        out_specs=P(None, ("group", "member"), None, None),
        check_vma=False,
    )
```

```python
import jax
import jax.numpy as jnp
from jax import lax
from jax.sharding import PartitionSpec as P

BLOCK = 512
EXCITE = 128
OWNERS = 4
DELAYS = 2
STEPS = 3


def shifted(x, axis, n, k):
    return lax.ppermute(x, axis, [(i, (i + k) % n) for i in range(n)])


def shift_gather(x, axis, n):
    return [x] + [shifted(x, axis, n, k) for k in range(1, n)]


def pick(pieces, index):
    if len(pieces) > 8:
        return jnp.take(jnp.stack(pieces), index, axis=0)
    chosen = index[:, None] == jnp.arange(len(pieces), dtype=index.dtype)[None, :]
    spread = (slice(None),) + (None,) * pieces[0].ndim
    total = None
    for k, piece in enumerate(pieces):
        term = jnp.where(chosen[:, k][spread], piece[None], jnp.zeros_like(piece)[None])
        total = term if total is None else total + term
    return total


def body(tile_values, tile_lists, owner_map, inverses, excitations, history):
    members = lax.axis_size("member")
    groups = lax.axis_size("group")
    group_blocks = members // OWNERS
    share = EXCITE // OWNERS
    group_here = lax.axis_index("group")
    member_here = lax.axis_index("member")
    owners = owner_map[0]
    member_ids = jnp.arange(members, dtype=jnp.int32)
    matches = owners[:, None] == member_ids[None, :]
    slot_of_member = jnp.sum(jnp.where(matches, member_ids[:, None], 0), axis=0)
    owner_shift = (member_here - owners) % members
    send_slot = jnp.take(slot_of_member, (member_here + member_ids) % members)

    lists_by_shift = jnp.stack(shift_gather(tile_lists, "group", groups))
    group_ids = jnp.arange(groups, dtype=jnp.int32)
    ahead = jnp.take(lists_by_shift, (groups - group_ids) % groups, axis=0)
    wanted = (ahead[:, :, 0] // group_blocks == group_here) & (ahead[:, :, 2] > 0)
    want_block = jnp.sum(jnp.where(wanted, ahead[:, :, 0] % group_blocks, 0), axis=1)
    want_delay = jnp.sum(jnp.where(wanted, ahead[:, :, 2], 0), axis=1)
    block_ids = jnp.arange(group_blocks, dtype=jnp.int32)
    which_block = want_block[:, None] == block_ids[None, :]
    from_near = which_block & (want_delay[:, None] == 1)
    from_far = which_block & (want_delay[:, None] == 2)

    source_group = tile_lists[:, 0] // group_blocks
    observer_local = tile_lists[:, 1] % group_blocks
    delays_here = tile_lists[:, 2]
    source_shift = (group_here - source_group) % groups

    hist_pieces = shift_gather(history[:, 0], "member", members)
    hist_placed = pick(hist_pieces, owner_shift)
    blocks = [
        hist_placed[:, t].reshape(group_blocks, EXCITE, BLOCK) for t in range(DELAYS)
    ]
    results = []
    for step in range(STEPS):
        near = blocks[DELAYS + step - 1]
        far = blocks[DELAYS + step - 2]
        outgoing = None
        for block in range(group_blocks):
            term = jnp.where(from_near[:, block, None, None], near[block][None], 0) + jnp.where(
                from_far[:, block, None, None], far[block][None], 0
            )
            outgoing = term if outgoing is None else outgoing + term
        received = [outgoing[0]] + [
            shifted(outgoing[k], "group", groups, k) for k in range(1, groups)
        ]
        blocks_in = pick(received, source_shift)
        terms = jnp.einsum(
            "kes,kso->keo", blocks_in, tile_values, preferred_element_type=jnp.float32
        )
        partial_sums = []
        for block in range(group_blocks):
            chosen = (observer_local == block) & (delays_here > 0)
            partial_sums.append(
                jnp.sum(jnp.where(chosen[:, None, None], terms, 0.0), axis=0)
            )
        slots = jnp.stack(partial_sums).astype(jnp.bfloat16).reshape(members, share, BLOCK)
        sent = pick([slots[s] for s in range(members)], send_slot)
        field = sent[0].astype(jnp.float32)
        for k in range(1, members):
            field = field + shifted(sent[k], "member", members, k).astype(jnp.float32)
        residual = (excitations[step, 0] - field).astype(jnp.bfloat16)
        current = jnp.dot(residual, inverses[0], preferred_element_type=jnp.float32)
        results.append(current)
        if step + 1 < STEPS:
            pieces = shift_gather(current.astype(jnp.bfloat16), "member", members)
            blocks.append(pick(pieces, owner_shift).reshape(group_blocks, EXCITE, BLOCK))
    return jnp.stack(results)[:, None]


def solution(mesh):
    placed = (
        P(("group", "member"), None, None),
        P(("group", "member"), None),
        P("group", None),
        P(("group", "member"), None, None),
        P(None, ("group", "member"), None, None),
        P(None, ("group", "member"), None, None),
    )
    return jax.shard_map(
        body,
        mesh=mesh,
        in_specs=placed,
        out_specs=P(None, ("group", "member"), None, None),
        check_vma=False,
    )
```

```python
import jax
import jax.numpy as jnp
from jax import lax
from jax.sharding import PartitionSpec as P

BLOCK = 512
EXCITE = 128
OWNERS = 4
DELAYS = 2
STEPS = 3


def shifted(x, axis, n, k):
    return lax.ppermute(x, axis, [(i, (i + k) % n) for i in range(n)])


def shift_gather(x, axis, n):
    return [x] + [shifted(x, axis, n, k) for k in range(1, n)]


def pick(pieces, index):
    if len(pieces) > 8:
        return jnp.take(jnp.stack(pieces), index, axis=0)
    chosen = index[:, None] == jnp.arange(len(pieces), dtype=index.dtype)[None, :]
    spread = (slice(None),) + (None,) * pieces[0].ndim
    total = None
    for k, piece in enumerate(pieces):
        term = jnp.where(chosen[:, k][spread], piece[None], jnp.zeros_like(piece)[None])
        total = term if total is None else total + term
    return total


def body(tile_values, tile_lists, owner_map, inverses, excitations, history):
    members = lax.axis_size("member")
    groups = lax.axis_size("group")
    group_blocks = members // OWNERS
    share = EXCITE // OWNERS
    group_here = lax.axis_index("group")
    member_here = lax.axis_index("member")
    owners = owner_map[0]
    member_ids = jnp.arange(members, dtype=jnp.int32)
    matches = owners[:, None] == member_ids[None, :]
    slot_of_member = jnp.sum(jnp.where(matches, member_ids[:, None], 0), axis=0)
    owner_shift = (member_here - owners) % members
    send_slot = jnp.take(slot_of_member, (member_here + member_ids) % members)

    lists_by_shift = jnp.stack(shift_gather(tile_lists, "group", groups))
    group_ids = jnp.arange(groups, dtype=jnp.int32)
    ahead = jnp.take(lists_by_shift, (groups - group_ids) % groups, axis=0)
    wanted = (ahead[:, :, 0] // group_blocks == group_here) & (ahead[:, :, 2] > 0)
    want_block = jnp.sum(jnp.where(wanted, ahead[:, :, 0] % group_blocks, 0), axis=1)
    want_delay = jnp.sum(jnp.where(wanted, ahead[:, :, 2], 0), axis=1)
    block_ids = jnp.arange(group_blocks, dtype=jnp.int32)
    which_block = want_block[:, None] == block_ids[None, :]
    from_near = which_block & (want_delay[:, None] == 1)
    from_far = which_block & (want_delay[:, None] == 2)

    source_group = tile_lists[:, 0] // group_blocks
    observer_local = tile_lists[:, 1] % group_blocks
    delays_here = tile_lists[:, 2]
    source_shift = (group_here - source_group) % groups

    hist_pieces = shift_gather(history[:, 0], "member", members)
    hist_placed = pick(hist_pieces, owner_shift)
    blocks = [
        hist_placed[:, t].reshape(group_blocks, EXCITE, BLOCK) for t in range(DELAYS)
    ]
    results = []
    for step in range(STEPS):
        near = blocks[DELAYS + step - 1]
        far = blocks[DELAYS + step - 2]
        outgoing = None
        for block in range(group_blocks):
            term = jnp.where(from_near[:, block, None, None], near[block][None], 0) + jnp.where(
                from_far[:, block, None, None], far[block][None], 0
            )
            outgoing = term if outgoing is None else outgoing + term
        received = [outgoing[0]] + [
            shifted(outgoing[k], "group", groups, k) for k in range(1, groups)
        ]
        blocks_in = pick(received, source_shift)
        terms = jnp.einsum(
            "kes,kso->keo", blocks_in, tile_values, preferred_element_type=jnp.float32
        )
        partial_sums = []
        for block in range(group_blocks):
            chosen = (observer_local == block) & (delays_here > 0)
            partial_sums.append(
                jnp.sum(jnp.where(chosen[:, None, None], terms, 0.0), axis=0)
            )
        slots = jnp.stack(partial_sums).astype(jnp.bfloat16).reshape(members, share, BLOCK)
        sent = pick([slots[s] for s in range(members)], slot_of_member)
        got = lax.all_to_all(sent, "member", 0, 0, tiled=True)
        field = jnp.sum(got.astype(jnp.float32), axis=0)
        residual = (excitations[step, 0] - field).astype(jnp.bfloat16)
        current = jnp.dot(residual, inverses[0], preferred_element_type=jnp.float32)
        results.append(current)
        if step + 1 < STEPS:
            spread = jnp.broadcast_to(current.astype(jnp.bfloat16)[None], (members, share, BLOCK))
            got = lax.all_to_all(spread, "member", 0, 0, tiled=True)
            placed = pick([got[m] for m in range(members)], owners)
            blocks.append(placed.reshape(group_blocks, EXCITE, BLOCK))
    return jnp.stack(results)[:, None]


def solution(mesh):
    placed = (
        P(("group", "member"), None, None),
        P(("group", "member"), None),
        P("group", None),
        P(("group", "member"), None, None),
        P(None, ("group", "member"), None, None),
        P(None, ("group", "member"), None, None),
    )
    return jax.shard_map(
        body,
        mesh=mesh,
        in_specs=placed,
        out_specs=P(None, ("group", "member"), None, None),
        check_vma=False,
    )
```

```python
import jax
import jax.numpy as jnp
from jax import lax
from jax.sharding import PartitionSpec as P

BLOCK = 512
EXCITE = 128
OWNERS = 4
DELAYS = 2
STEPS = 3
WHOLE_TIME_DEVICES = 64


def shifted(x, axis, n, k):
    return lax.ppermute(x, axis, [(i, (i + k) % n) for i in range(n)])


def shift_gather(x, axis, n):
    return [x] + [shifted(x, axis, n, k) for k in range(1, n)]


def pick(pieces, index):
    if len(pieces) > 8:
        return jnp.take(jnp.stack(pieces), index, axis=0)
    chosen = index[:, None] == jnp.arange(len(pieces), dtype=index.dtype)[None, :]
    spread = (slice(None),) + (None,) * pieces[0].ndim
    total = None
    for k, piece in enumerate(pieces):
        term = jnp.where(chosen[:, k][spread], piece[None], jnp.zeros_like(piece)[None])
        total = term if total is None else total + term
    return total


def member_gather(x, members):
    spread = jnp.broadcast_to(x[None], (members,) + x.shape)
    return lax.all_to_all(spread, "member", 0, 0, tiled=True)


def body(tile_values, tile_lists, owner_map, inverses, excitations, history):
    members = lax.axis_size("member")
    groups = lax.axis_size("group")
    group_blocks = members // OWNERS
    share = EXCITE // OWNERS
    group_here = lax.axis_index("group")
    member_here = lax.axis_index("member")
    owners = owner_map[0]
    member_ids = jnp.arange(members, dtype=jnp.int32)
    group_ids = jnp.arange(groups, dtype=jnp.int32)
    block_ids = jnp.arange(group_blocks, dtype=jnp.int32)
    matches = owners[:, None] == member_ids[None, :]
    slot_of_member = jnp.sum(jnp.where(matches, member_ids[:, None], 0), axis=0)
    tiles_here = tile_lists.shape[0]

    source_group = tile_lists[:, 0] // group_blocks
    source_local = tile_lists[:, 0] % group_blocks
    observer_local = tile_lists[:, 1] % group_blocks
    delays_here = tile_lists[:, 2]
    source_shift = (group_here - source_group) % groups
    whole_time = members * groups <= WHOLE_TIME_DEVICES

    if whole_time:
        maps_by_shift = jnp.stack(shift_gather(owners, "group", groups))
        slots_wanted = OWNERS * source_local[:, None] + jnp.arange(OWNERS, dtype=jnp.int32)[None, :]
        owner_wanted = jnp.take_along_axis(maps_by_shift[source_shift], slots_wanted, axis=1)
        flat_wanted = owner_wanted * groups + source_shift[:, None]
        selector = (
            flat_wanted[:, :, None] == jnp.arange(members * groups, dtype=jnp.int32)[None, None, :]
        ).astype(jnp.bfloat16)

        def rows_for_tiles(gathered):
            flat = gathered.reshape(members * groups, share * BLOCK)
            rows = jnp.einsum("iqf,fx->iqx", selector, flat, preferred_element_type=jnp.float32)
            return rows.astype(jnp.bfloat16).reshape(tiles_here, EXCITE, BLOCK)

        def spread_currents(piece):
            across = jnp.stack(shift_gather(piece, "group", groups))
            return member_gather(across, members)

        hist = spread_currents(history[:, 0])
        rows_at = [rows_for_tiles(hist[:, :, t]) for t in range(DELAYS)]
    else:
        owner_shift = (member_here - owners) % members
        lists_by_shift = jnp.stack(shift_gather(tile_lists, "group", groups))
        ahead = jnp.take(lists_by_shift, (groups - group_ids) % groups, axis=0)
        wanted = (ahead[:, :, 0] // group_blocks == group_here) & (ahead[:, :, 2] > 0)
        want_block = jnp.sum(jnp.where(wanted, ahead[:, :, 0] % group_blocks, 0), axis=1)
        want_delay = jnp.sum(jnp.where(wanted, ahead[:, :, 2], 0), axis=1)
        which_block = want_block[:, None] == block_ids[None, :]
        from_near = which_block & (want_delay[:, None] == 1)
        from_far = which_block & (want_delay[:, None] == 2)
        hist = member_gather(history[:, 0], members)
        hist_placed = pick([hist[m] for m in range(members)], owners)
        blocks = [
            hist_placed[:, t].reshape(group_blocks, EXCITE, BLOCK) for t in range(DELAYS)
        ]

    results = []
    for step in range(STEPS):
        if whole_time:
            blocks_in = jnp.where(
                (delays_here == 1)[:, None, None], rows_at[DELAYS + step - 1], rows_at[DELAYS + step - 2]
            )
        else:
            near = blocks[DELAYS + step - 1]
            far = blocks[DELAYS + step - 2]
            outgoing = None
            for block in range(group_blocks):
                term = jnp.where(from_near[:, block, None, None], near[block][None], 0) + jnp.where(
                    from_far[:, block, None, None], far[block][None], 0
                )
                outgoing = term if outgoing is None else outgoing + term
            received = [outgoing[0]] + [
                shifted(outgoing[k], "group", groups, k) for k in range(1, groups)
            ]
            blocks_in = pick(received, source_shift)
        terms = jnp.einsum(
            "kes,kso->keo", blocks_in, tile_values, preferred_element_type=jnp.float32
        )
        partial_sums = []
        for block in range(group_blocks):
            chosen = (observer_local == block) & (delays_here > 0)
            partial_sums.append(
                jnp.sum(jnp.where(chosen[:, None, None], terms, 0.0), axis=0)
            )
        slots = jnp.stack(partial_sums).astype(jnp.bfloat16).reshape(members, share, BLOCK)
        sent = pick([slots[s] for s in range(members)], slot_of_member)
        got = lax.all_to_all(sent, "member", 0, 0, tiled=True)
        field = jnp.sum(got.astype(jnp.float32), axis=0)
        residual = (excitations[step, 0] - field).astype(jnp.bfloat16)
        current = jnp.dot(residual, inverses[0], preferred_element_type=jnp.float32)
        results.append(current)
        if step + 1 < STEPS:
            piece = current.astype(jnp.bfloat16)
            if whole_time:
                rows_at.append(rows_for_tiles(spread_currents(piece)))
            else:
                got = member_gather(piece, members)
                placed = pick([got[m] for m in range(members)], owners)
                blocks.append(placed.reshape(group_blocks, EXCITE, BLOCK))
    return jnp.stack(results)[:, None]


def solution(mesh):
    placed = (
        P(("group", "member"), None, None),
        P(("group", "member"), None),
        P("group", None),
        P(("group", "member"), None, None),
        P(None, ("group", "member"), None, None),
        P(None, ("group", "member"), None, None),
    )
    return jax.shard_map(
        body,
        mesh=mesh,
        in_specs=placed,
        out_specs=P(None, ("group", "member"), None, None),
        check_vma=False,
    )
```

```python
import jax
import jax.numpy as jnp
from jax import lax
from jax.sharding import PartitionSpec as P

BLOCK = 512
EXCITE = 128
OWNERS = 4
DELAYS = 2
STEPS = 3


def shifted(x, axis, n, k):
    return lax.ppermute(x, axis, [(i, (i + k) % n) for i in range(n)])


def shift_gather(x, axis, n):
    return [x] + [shifted(x, axis, n, k) for k in range(1, n)]


def pick(pieces, index):
    if len(pieces) > 8:
        return jnp.take(jnp.stack(pieces), index, axis=0)
    chosen = index[:, None] == jnp.arange(len(pieces), dtype=index.dtype)[None, :]
    spread = (slice(None),) + (None,) * pieces[0].ndim
    total = None
    for k, piece in enumerate(pieces):
        term = jnp.where(chosen[:, k][spread], piece[None], jnp.zeros_like(piece)[None])
        total = term if total is None else total + term
    return total


def body(tile_values, tile_lists, owner_map, inverses, excitations, history):
    members = lax.axis_size("member")
    groups = lax.axis_size("group")
    group_blocks = members // OWNERS
    share = EXCITE // OWNERS
    group_here = lax.axis_index("group")
    member_here = lax.axis_index("member")
    owners = owner_map[0]
    member_ids = jnp.arange(members, dtype=jnp.int32)
    matches = owners[:, None] == member_ids[None, :]
    slot_of_member = jnp.sum(jnp.where(matches, member_ids[:, None], 0), axis=0)
    send_slot = jnp.take(slot_of_member, (member_here + member_ids) % members)

    lists_by_shift = jnp.stack(shift_gather(tile_lists, "group", groups))
    group_ids = jnp.arange(groups, dtype=jnp.int32)
    ahead = jnp.take(lists_by_shift, (groups - group_ids) % groups, axis=0)
    wanted = (ahead[:, :, 0] // group_blocks == group_here) & (ahead[:, :, 2] > 0)
    want_block = jnp.sum(jnp.where(wanted, ahead[:, :, 0] % group_blocks, 0), axis=1)
    want_delay = jnp.sum(jnp.where(wanted, ahead[:, :, 2], 0), axis=1)
    block_ids = jnp.arange(group_blocks, dtype=jnp.int32)
    which_block = want_block[:, None] == block_ids[None, :]
    from_near = which_block & (want_delay[:, None] == 1)
    from_far = which_block & (want_delay[:, None] == 2)

    source_group = tile_lists[:, 0] // group_blocks
    observer_local = tile_lists[:, 1] % group_blocks
    delays_here = tile_lists[:, 2]
    source_shift = (group_here - source_group) % groups

    spread_hist = jnp.broadcast_to(history[:, 0][None], (members,) + history[:, 0].shape)
    hist_got = lax.all_to_all(spread_hist, "member", 0, 0, tiled=True)
    hist_placed = pick([hist_got[m] for m in range(members)], owners)
    blocks = [
        hist_placed[:, t].reshape(group_blocks, EXCITE, BLOCK) for t in range(DELAYS)
    ]
    results = []
    for step in range(STEPS):
        near = blocks[DELAYS + step - 1]
        far = blocks[DELAYS + step - 2]
        outgoing = None
        for block in range(group_blocks):
            term = jnp.where(from_near[:, block, None, None], near[block][None], 0) + jnp.where(
                from_far[:, block, None, None], far[block][None], 0
            )
            outgoing = term if outgoing is None else outgoing + term
        received = [outgoing[0]] + [
            shifted(outgoing[k], "group", groups, k) for k in range(1, groups)
        ]
        blocks_in = pick(received, source_shift)
        terms = jnp.einsum(
            "kes,kso->keo", blocks_in, tile_values, preferred_element_type=jnp.float32
        )
        partial_sums = []
        for block in range(group_blocks):
            chosen = (observer_local == block) & (delays_here > 0)
            partial_sums.append(
                jnp.sum(jnp.where(chosen[:, None, None], terms, 0.0), axis=0)
            )
        slots = jnp.stack(partial_sums).astype(jnp.bfloat16).reshape(members, share, BLOCK)
        sent = pick([slots[s] for s in range(members)], slot_of_member)
        got = lax.all_to_all(sent, "member", 0, 0, tiled=True)
        field = jnp.sum(got.astype(jnp.float32), axis=0)
        residual = (excitations[step, 0] - field).astype(jnp.bfloat16)
        current = jnp.dot(residual, inverses[0], preferred_element_type=jnp.float32)
        results.append(current)
        if step + 1 < STEPS:
            spread = jnp.broadcast_to(current.astype(jnp.bfloat16)[None], (members, share, BLOCK))
            got = lax.all_to_all(spread, "member", 0, 0, tiled=True)
            placed = pick([got[m] for m in range(members)], owners)
            blocks.append(placed.reshape(group_blocks, EXCITE, BLOCK))
    return jnp.stack(results)[:, None]


def solution(mesh):
    placed = (
        P(("group", "member"), None, None),
        P(("group", "member"), None),
        P("group", None),
        P(("group", "member"), None, None),
        P(None, ("group", "member"), None, None),
        P(None, ("group", "member"), None, None),
    )
    return jax.shard_map(
        body,
        mesh=mesh,
        in_specs=placed,
        out_specs=P(None, ("group", "member"), None, None),
        check_vma=False,
    )
```

```python
import jax
import jax.numpy as jnp
from jax import lax
from jax.sharding import PartitionSpec as P

BLOCK = 512
EXCITE = 128
OWNERS = 4
DELAYS = 2
STEPS = 3


def shifted(x, axis, n, k):
    return lax.ppermute(x, axis, [(i, (i + k) % n) for i in range(n)])


def shift_gather(x, axis, n):
    return [x] + [shifted(x, axis, n, k) for k in range(1, n)]


def pick(pieces, index):
    if len(pieces) > 8:
        return jnp.take(jnp.stack(pieces), index, axis=0)
    chosen = index[:, None] == jnp.arange(len(pieces), dtype=index.dtype)[None, :]
    spread = (slice(None),) + (None,) * pieces[0].ndim
    total = None
    for k, piece in enumerate(pieces):
        term = jnp.where(chosen[:, k][spread], piece[None], jnp.zeros_like(piece)[None])
        total = term if total is None else total + term
    return total


def body(tile_values, tile_lists, owner_map, inverses, excitations, history):
    members = lax.axis_size("member")
    groups = lax.axis_size("group")
    group_blocks = members // OWNERS
    share = EXCITE // OWNERS
    group_here = lax.axis_index("group")
    member_here = lax.axis_index("member")
    owners = owner_map[0]
    member_ids = jnp.arange(members, dtype=jnp.int32)
    matches = owners[:, None] == member_ids[None, :]
    slot_of_member = jnp.sum(jnp.where(matches, member_ids[:, None], 0), axis=0)
    send_slot = jnp.take(slot_of_member, (member_here + member_ids) % members)

    lists_by_shift = jnp.stack(shift_gather(tile_lists, "group", groups))
    group_ids = jnp.arange(groups, dtype=jnp.int32)
    ahead = jnp.take(lists_by_shift, (groups - group_ids) % groups, axis=0)
    wanted = (ahead[:, :, 0] // group_blocks == group_here) & (ahead[:, :, 2] > 0)
    want_block = jnp.sum(jnp.where(wanted, ahead[:, :, 0] % group_blocks, 0), axis=1)
    want_delay = jnp.sum(jnp.where(wanted, ahead[:, :, 2], 0), axis=1)
    block_ids = jnp.arange(group_blocks, dtype=jnp.int32)
    which_block = want_block[:, None] == block_ids[None, :]
    from_near = which_block & (want_delay[:, None] == 1)
    from_far = which_block & (want_delay[:, None] == 2)

    source_group = tile_lists[:, 0] // group_blocks
    observer_local = tile_lists[:, 1] % group_blocks
    delays_here = tile_lists[:, 2]
    source_shift = (group_here - source_group) % groups

    spread_hist = jnp.broadcast_to(history[:, 0][None], (members,) + history[:, 0].shape)
    hist_got = lax.all_to_all(spread_hist, "member", 0, 0, tiled=True)
    hist_placed = pick([hist_got[m] for m in range(members)], owners)
    blocks = [
        hist_placed[:, t].reshape(group_blocks, EXCITE, BLOCK) for t in range(DELAYS)
    ]
    results = []
    for step in range(STEPS):
        near = blocks[DELAYS + step - 1]
        far = blocks[DELAYS + step - 2]
        outgoing = None
        for block in range(group_blocks):
            term = jnp.where(from_near[:, block, None, None], near[block][None], 0) + jnp.where(
                from_far[:, block, None, None], far[block][None], 0
            )
            outgoing = term if outgoing is None else outgoing + term
        half = EXCITE // 2
        received = [outgoing[0]] + [
            jnp.concatenate(
                [
                    shifted(outgoing[k, :half], "group", groups, k),
                    shifted(outgoing[k, half:], "group", groups, k),
                ],
                axis=0,
            )
            for k in range(1, groups)
        ]
        blocks_in = pick(received, source_shift)
        terms = jnp.einsum(
            "kes,kso->keo", blocks_in, tile_values, preferred_element_type=jnp.float32
        )
        partial_sums = []
        for block in range(group_blocks):
            chosen = (observer_local == block) & (delays_here > 0)
            partial_sums.append(
                jnp.sum(jnp.where(chosen[:, None, None], terms, 0.0), axis=0)
            )
        slots = jnp.stack(partial_sums).astype(jnp.bfloat16).reshape(members, share, BLOCK)
        sent = pick([slots[s] for s in range(members)], slot_of_member)
        got = lax.all_to_all(sent, "member", 0, 0, tiled=True)
        field = jnp.sum(got.astype(jnp.float32), axis=0)
        residual = (excitations[step, 0] - field).astype(jnp.bfloat16)
        current = jnp.dot(residual, inverses[0], preferred_element_type=jnp.float32)
        results.append(current)
        if step + 1 < STEPS:
            spread = jnp.broadcast_to(current.astype(jnp.bfloat16)[None], (members, share, BLOCK))
            got = lax.all_to_all(spread, "member", 0, 0, tiled=True)
            placed = pick([got[m] for m in range(members)], owners)
            blocks.append(placed.reshape(group_blocks, EXCITE, BLOCK))
    return jnp.stack(results)[:, None]


def solution(mesh):
    placed = (
        P(("group", "member"), None, None),
        P(("group", "member"), None),
        P("group", None),
        P(("group", "member"), None, None),
        P(None, ("group", "member"), None, None),
        P(None, ("group", "member"), None, None),
    )
    return jax.shard_map(
        body,
        mesh=mesh,
        in_specs=placed,
        out_specs=P(None, ("group", "member"), None, None),
        check_vma=False,
    )
```

```python
import jax
import jax.numpy as jnp
from jax import lax
from jax.sharding import PartitionSpec as P

BLOCK = 512
EXCITE = 128
OWNERS = 4
DELAYS = 2
STEPS = 3


def shifted(x, axis, n, k):
    return lax.ppermute(x, axis, [(i, (i + k) % n) for i in range(n)])


def shift_gather(x, axis, n):
    return [x] + [shifted(x, axis, n, k) for k in range(1, n)]


def pick(pieces, index):
    if len(pieces) > 8:
        return jnp.take(jnp.stack(pieces), index, axis=0)
    chosen = index[:, None] == jnp.arange(len(pieces), dtype=index.dtype)[None, :]
    spread = (slice(None),) + (None,) * pieces[0].ndim
    total = None
    for k, piece in enumerate(pieces):
        term = jnp.where(chosen[:, k][spread], piece[None], jnp.zeros_like(piece)[None])
        total = term if total is None else total + term
    return total


def body(tile_values, tile_lists, owner_map, inverses, excitations, history):
    members = lax.axis_size("member")
    groups = lax.axis_size("group")
    group_blocks = members // OWNERS
    share = EXCITE // OWNERS
    group_here = lax.axis_index("group")
    member_here = lax.axis_index("member")
    owners = owner_map[0]
    member_ids = jnp.arange(members, dtype=jnp.int32)
    matches = owners[:, None] == member_ids[None, :]
    slot_of_member = jnp.sum(jnp.where(matches, member_ids[:, None], 0), axis=0)
    send_slot = jnp.take(slot_of_member, (member_here + member_ids) % members)

    lists_by_shift = jnp.stack(shift_gather(tile_lists, "group", groups))
    group_ids = jnp.arange(groups, dtype=jnp.int32)
    ahead = jnp.take(lists_by_shift, (groups - group_ids) % groups, axis=0)
    wanted = (ahead[:, :, 0] // group_blocks == group_here) & (ahead[:, :, 2] > 0)
    want_block = jnp.sum(jnp.where(wanted, ahead[:, :, 0] % group_blocks, 0), axis=1)
    want_delay = jnp.sum(jnp.where(wanted, ahead[:, :, 2], 0), axis=1)
    block_ids = jnp.arange(group_blocks, dtype=jnp.int32)
    which_block = want_block[:, None] == block_ids[None, :]
    from_near = which_block & (want_delay[:, None] == 1)
    from_far = which_block & (want_delay[:, None] == 2)

    source_group = tile_lists[:, 0] // group_blocks
    observer_local = tile_lists[:, 1] % group_blocks
    delays_here = tile_lists[:, 2]
    source_shift = (group_here - source_group) % groups

    hist_got = lax.all_gather(history[:, 0], "member", axis=0, tiled=False)
    hist_placed = pick([hist_got[m] for m in range(members)], owners)
    blocks = [
        hist_placed[:, t].reshape(group_blocks, EXCITE, BLOCK) for t in range(DELAYS)
    ]
    results = []
    for step in range(STEPS):
        near = blocks[DELAYS + step - 1]
        far = blocks[DELAYS + step - 2]
        outgoing = None
        for block in range(group_blocks):
            term = jnp.where(from_near[:, block, None, None], near[block][None], 0) + jnp.where(
                from_far[:, block, None, None], far[block][None], 0
            )
            outgoing = term if outgoing is None else outgoing + term
        received = [outgoing[0]] + [
            shifted(outgoing[k], "group", groups, k) for k in range(1, groups)
        ]
        blocks_in = pick(received, source_shift)
        terms = jnp.einsum(
            "kes,kso->keo", blocks_in, tile_values, preferred_element_type=jnp.float32
        )
        partial_sums = []
        for block in range(group_blocks):
            chosen = (observer_local == block) & (delays_here > 0)
            partial_sums.append(
                jnp.sum(jnp.where(chosen[:, None, None], terms, 0.0), axis=0)
            )
        slots = jnp.stack(partial_sums).astype(jnp.bfloat16).reshape(members, share, BLOCK)
        sent = pick([slots[s] for s in range(members)], slot_of_member)
        got = lax.all_to_all(sent, "member", 0, 0, tiled=True)
        field = jnp.sum(got.astype(jnp.float32), axis=0)
        residual = (excitations[step, 0] - field).astype(jnp.bfloat16)
        current = jnp.dot(residual, inverses[0], preferred_element_type=jnp.float32)
        results.append(current)
        if step + 1 < STEPS:
            got = lax.all_gather(current.astype(jnp.bfloat16), "member", axis=0, tiled=False)
            placed = pick([got[m] for m in range(members)], owners)
            blocks.append(placed.reshape(group_blocks, EXCITE, BLOCK))
    return jnp.stack(results)[:, None]


def solution(mesh):
    placed = (
        P(("group", "member"), None, None),
        P(("group", "member"), None),
        P("group", None),
        P(("group", "member"), None, None),
        P(None, ("group", "member"), None, None),
        P(None, ("group", "member"), None, None),
    )
    return jax.shard_map(
        body,
        mesh=mesh,
        in_specs=placed,
        out_specs=P(None, ("group", "member"), None, None),
        check_vma=False,
    )
```

```python
import jax
import jax.numpy as jnp
from jax import lax
from jax.sharding import PartitionSpec as P

BLOCK = 512
EXCITE = 128
OWNERS = 4
DELAYS = 2
STEPS = 3


def shifted(x, axis, n, k):
    return lax.ppermute(x, axis, [(i, (i + k) % n) for i in range(n)])


def shift_gather(x, axis, n):
    return [x] + [shifted(x, axis, n, k) for k in range(1, n)]


def pick(pieces, index):
    if len(pieces) > 8:
        return jnp.take(jnp.stack(pieces), index, axis=0)
    chosen = index[:, None] == jnp.arange(len(pieces), dtype=index.dtype)[None, :]
    spread = (slice(None),) + (None,) * pieces[0].ndim
    total = None
    for k, piece in enumerate(pieces):
        term = jnp.where(chosen[:, k][spread], piece[None], jnp.zeros_like(piece)[None])
        total = term if total is None else total + term
    return total


def body(tile_values, tile_lists, owner_map, inverses, excitations, history):
    members = lax.axis_size("member")
    groups = lax.axis_size("group")
    group_blocks = members // OWNERS
    share = EXCITE // OWNERS
    group_here = lax.axis_index("group")
    member_here = lax.axis_index("member")
    owners = owner_map[0]
    member_ids = jnp.arange(members, dtype=jnp.int32)
    matches = owners[:, None] == member_ids[None, :]
    slot_of_member = jnp.sum(jnp.where(matches, member_ids[:, None], 0), axis=0)
    send_slot = jnp.take(slot_of_member, (member_here + member_ids) % members)

    lists_by_shift = jnp.stack(shift_gather(tile_lists, "group", groups))
    group_ids = jnp.arange(groups, dtype=jnp.int32)
    ahead = jnp.take(lists_by_shift, (groups - group_ids) % groups, axis=0)
    wanted = (ahead[:, :, 0] // group_blocks == group_here) & (ahead[:, :, 2] > 0)
    want_block = jnp.sum(jnp.where(wanted, ahead[:, :, 0] % group_blocks, 0), axis=1)
    want_delay = jnp.sum(jnp.where(wanted, ahead[:, :, 2], 0), axis=1)
    block_ids = jnp.arange(group_blocks, dtype=jnp.int32)
    which_block = want_block[:, None] == block_ids[None, :]
    from_near = which_block & (want_delay[:, None] == 1)
    from_far = which_block & (want_delay[:, None] == 2)

    source_group = tile_lists[:, 0] // group_blocks
    observer_local = tile_lists[:, 1] % group_blocks
    delays_here = tile_lists[:, 2]
    source_shift = (group_here - source_group) % groups

    spread_hist = jnp.broadcast_to(history[:, 0][None], (members,) + history[:, 0].shape)
    hist_got = lax.all_to_all(spread_hist, "member", 0, 0, tiled=True)
    hist_placed = pick([hist_got[m] for m in range(members)], owners)
    blocks = [
        hist_placed[:, t].reshape(group_blocks, EXCITE, BLOCK) for t in range(DELAYS)
    ]
    results = []
    for step in range(STEPS):
        near = blocks[DELAYS + step - 1]
        far = blocks[DELAYS + step - 2]
        outgoing = None
        for block in range(group_blocks):
            term = jnp.where(from_near[:, block, None, None], near[block][None], 0) + jnp.where(
                from_far[:, block, None, None], far[block][None], 0
            )
            outgoing = term if outgoing is None else outgoing + term
        received = [outgoing[0]] + [
            shifted(outgoing[k], "group", groups, k) for k in range(1, groups)
        ]
        blocks_in = pick(received, source_shift)
        terms = jnp.einsum(
            "kes,kso->keo", blocks_in, tile_values, preferred_element_type=jnp.float32
        )
        partial_sums = []
        for block in range(group_blocks):
            chosen = (observer_local == block) & (delays_here > 0)
            partial_sums.append(
                jnp.sum(jnp.where(chosen[:, None, None], terms, 0.0), axis=0)
            )
        slots = jnp.stack(partial_sums).astype(jnp.bfloat16).reshape(members, share, BLOCK)
        sent = pick([slots[s] for s in range(members)], slot_of_member)
        got = lax.all_to_all(sent, "member", 0, 0, tiled=True)
        field = jnp.sum(got.astype(jnp.float32), axis=0)
        residual = (excitations[step, 0] - field).astype(jnp.bfloat16)
        current = jnp.dot(residual, inverses[0], preferred_element_type=jnp.float32)
        results.append(current)
        if step + 1 < STEPS:
            got = lax.all_gather(current.astype(jnp.bfloat16), "member", axis=0, tiled=False)
            placed = pick([got[m] for m in range(members)], owners)
            blocks.append(placed.reshape(group_blocks, EXCITE, BLOCK))
    return jnp.stack(results)[:, None]


def solution(mesh):
    placed = (
        P(("group", "member"), None, None),
        P(("group", "member"), None),
        P("group", None),
        P(("group", "member"), None, None),
        P(None, ("group", "member"), None, None),
        P(None, ("group", "member"), None, None),
    )
    return jax.shard_map(
        body,
        mesh=mesh,
        in_specs=placed,
        out_specs=P(None, ("group", "member"), None, None),
        check_vma=False,
    )
```

```python
import jax
import jax.numpy as jnp
from jax import lax
from jax.sharding import PartitionSpec as P

BLOCK = 512
EXCITE = 128
OWNERS = 4
DELAYS = 2
STEPS = 3


def shifted(x, axis, n, k):
    return lax.ppermute(x, axis, [(i, (i + k) % n) for i in range(n)])


def shift_gather(x, axis, n):
    return [x] + [shifted(x, axis, n, k) for k in range(1, n)]


def pick(pieces, index):
    if len(pieces) > 8:
        return jnp.take(jnp.stack(pieces), index, axis=0)
    chosen = index[:, None] == jnp.arange(len(pieces), dtype=index.dtype)[None, :]
    spread = (slice(None),) + (None,) * pieces[0].ndim
    total = None
    for k, piece in enumerate(pieces):
        term = jnp.where(chosen[:, k][spread], piece[None], jnp.zeros_like(piece)[None])
        total = term if total is None else total + term
    return total


def body(tile_values, tile_lists, owner_map, inverses, excitations, history):
    members = lax.axis_size("member")
    groups = lax.axis_size("group")
    group_blocks = members // OWNERS
    share = EXCITE // OWNERS
    group_here = lax.axis_index("group")
    member_here = lax.axis_index("member")
    owners = owner_map[0]
    member_ids = jnp.arange(members, dtype=jnp.int32)
    matches = owners[:, None] == member_ids[None, :]
    slot_of_member = jnp.sum(jnp.where(matches, member_ids[:, None], 0), axis=0)
    send_slot = jnp.take(slot_of_member, (member_here + member_ids) % members)

    lists_by_shift = jnp.stack(shift_gather(tile_lists, "group", groups))
    group_ids = jnp.arange(groups, dtype=jnp.int32)
    ahead = jnp.take(lists_by_shift, (groups - group_ids) % groups, axis=0)
    wanted = (ahead[:, :, 0] // group_blocks == group_here) & (ahead[:, :, 2] > 0)
    want_block = jnp.sum(jnp.where(wanted, ahead[:, :, 0] % group_blocks, 0), axis=1)
    want_delay = jnp.sum(jnp.where(wanted, ahead[:, :, 2], 0), axis=1)
    block_ids = jnp.arange(group_blocks, dtype=jnp.int32)
    which_block = want_block[:, None] == block_ids[None, :]
    from_near = which_block & (want_delay[:, None] == 1)
    from_far = which_block & (want_delay[:, None] == 2)

    source_group = tile_lists[:, 0] // group_blocks
    observer_local = tile_lists[:, 1] % group_blocks
    delays_here = tile_lists[:, 2]
    source_shift = (group_here - source_group) % groups

    spread_hist = jnp.broadcast_to(history[:, 0][None], (members,) + history[:, 0].shape)
    hist_got = lax.all_to_all(spread_hist, "member", 0, 0, tiled=True)
    hist_placed = pick([hist_got[m] for m in range(members)], owners)
    blocks = [
        hist_placed[:, t].reshape(group_blocks, EXCITE, BLOCK) for t in range(DELAYS)
    ]
    results = []
    for step in range(STEPS):
        near = blocks[DELAYS + step - 1]
        far = blocks[DELAYS + step - 2]
        def piece_for(k, near, far):
            total = None
            for block in range(group_blocks):
                term = jnp.where(from_near[k, block], near[block], 0) + jnp.where(
                    from_far[k, block], far[block], 0
                )
                total = term if total is None else total + term
            return total

        middle = groups // 2
        first = piece_for(middle, near, far)
        arrived = {middle: shifted(first, "group", groups, middle)}
        first, near, far = lax.optimization_barrier((first, near, far))
        for k in range(1, groups):
            if k != middle:
                arrived[k] = shifted(piece_for(k, near, far), "group", groups, k)
        received = [piece_for(0, near, far)] + [arrived[k] for k in range(1, groups)]
        blocks_in = pick(received, source_shift)
        terms = jnp.einsum(
            "kes,kso->keo", blocks_in, tile_values, preferred_element_type=jnp.float32
        )
        partial_sums = []
        for block in range(group_blocks):
            chosen = (observer_local == block) & (delays_here > 0)
            partial_sums.append(
                jnp.sum(jnp.where(chosen[:, None, None], terms, 0.0), axis=0)
            )
        slots = jnp.stack(partial_sums).astype(jnp.bfloat16).reshape(members, share, BLOCK)
        sent = pick([slots[s] for s in range(members)], slot_of_member)
        got = lax.all_to_all(sent, "member", 0, 0, tiled=True)
        field = jnp.sum(got.astype(jnp.float32), axis=0)
        residual = (excitations[step, 0] - field).astype(jnp.bfloat16)
        current = jnp.dot(residual, inverses[0], preferred_element_type=jnp.float32)
        results.append(current)
        if step + 1 < STEPS:
            spread = jnp.broadcast_to(current.astype(jnp.bfloat16)[None], (members, share, BLOCK))
            got = lax.all_to_all(spread, "member", 0, 0, tiled=True)
            placed = pick([got[m] for m in range(members)], owners)
            blocks.append(placed.reshape(group_blocks, EXCITE, BLOCK))
    return jnp.stack(results)[:, None]


def solution(mesh):
    placed = (
        P(("group", "member"), None, None),
        P(("group", "member"), None),
        P("group", None),
        P(("group", "member"), None, None),
        P(None, ("group", "member"), None, None),
        P(None, ("group", "member"), None, None),
    )
    return jax.shard_map(
        body,
        mesh=mesh,
        in_specs=placed,
        out_specs=P(None, ("group", "member"), None, None),
        check_vma=False,
    )
```

```python
import jax
import jax.numpy as jnp
from jax import lax
from jax.sharding import PartitionSpec as P

BLOCK = 512
EXCITE = 128
OWNERS = 4
DELAYS = 2
STEPS = 3


def shifted(x, axis, n, k):
    return lax.ppermute(x, axis, [(i, (i + k) % n) for i in range(n)])


def shift_gather(x, axis, n):
    return [x] + [shifted(x, axis, n, k) for k in range(1, n)]


def pick(pieces, index):
    if len(pieces) > 8:
        return jnp.take(jnp.stack(pieces), index, axis=0)
    chosen = index[:, None] == jnp.arange(len(pieces), dtype=index.dtype)[None, :]
    spread = (slice(None),) + (None,) * pieces[0].ndim
    total = None
    for k, piece in enumerate(pieces):
        term = jnp.where(chosen[:, k][spread], piece[None], jnp.zeros_like(piece)[None])
        total = term if total is None else total + term
    return total


def body(tile_values, tile_lists, owner_map, inverses, excitations, history):
    members = lax.axis_size("member")
    groups = lax.axis_size("group")
    group_blocks = members // OWNERS
    share = EXCITE // OWNERS
    group_here = lax.axis_index("group")
    member_here = lax.axis_index("member")
    owners = owner_map[0]
    member_ids = jnp.arange(members, dtype=jnp.int32)
    matches = owners[:, None] == member_ids[None, :]
    slot_of_member = jnp.sum(jnp.where(matches, member_ids[:, None], 0), axis=0)
    send_slot = jnp.take(slot_of_member, (member_here + member_ids) % members)

    lists_by_shift = jnp.stack(shift_gather(tile_lists, "group", groups))
    group_ids = jnp.arange(groups, dtype=jnp.int32)
    ahead = jnp.take(lists_by_shift, (groups - group_ids) % groups, axis=0)
    wanted = (ahead[:, :, 0] // group_blocks == group_here) & (ahead[:, :, 2] > 0)
    want_block = jnp.sum(jnp.where(wanted, ahead[:, :, 0] % group_blocks, 0), axis=1)
    want_delay = jnp.sum(jnp.where(wanted, ahead[:, :, 2], 0), axis=1)
    block_ids = jnp.arange(group_blocks, dtype=jnp.int32)
    which_block = want_block[:, None] == block_ids[None, :]
    from_near = which_block & (want_delay[:, None] == 1)
    from_far = which_block & (want_delay[:, None] == 2)

    source_group = tile_lists[:, 0] // group_blocks
    observer_local = tile_lists[:, 1] % group_blocks
    delays_here = tile_lists[:, 2]
    source_shift = (group_here - source_group) % groups

    spread_hist = jnp.broadcast_to(history[:, 0][None], (members,) + history[:, 0].shape)
    hist_got = lax.all_to_all(spread_hist, "member", 0, 0, tiled=True)
    hist_placed = pick([hist_got[m] for m in range(members)], owners)
    blocks = [
        hist_placed[:, t].reshape(group_blocks, EXCITE, BLOCK) for t in range(DELAYS)
    ]
    results = []
    for step in range(STEPS):
        near = blocks[DELAYS + step - 1]
        far = blocks[DELAYS + step - 2]
        def pieces_for(rows, take_near, take_far):
            total = None
            for block in range(group_blocks):
                term = jnp.where(take_near[rows, block, None, None], near[block][None], 0) + jnp.where(
                    take_far[rows, block, None, None], far[block][None], 0
                )
                total = term if total is None else total + term
            return total

        middle = groups // 2
        first = pieces_for(slice(middle, middle + 1), from_near, from_far)[0]
        arrived = {middle: shifted(first, "group", groups, middle)}
        first, take_near, take_far = lax.optimization_barrier((first, from_near, from_far))
        outgoing = pieces_for(slice(None), take_near, take_far)
        for k in range(1, groups):
            if k != middle:
                arrived[k] = shifted(outgoing[k], "group", groups, k)
        received = [outgoing[0]] + [arrived[k] for k in range(1, groups)]
        blocks_in = pick(received, source_shift)
        terms = jnp.einsum(
            "kes,kso->keo", blocks_in, tile_values, preferred_element_type=jnp.float32
        )
        partial_sums = []
        for block in range(group_blocks):
            chosen = (observer_local == block) & (delays_here > 0)
            partial_sums.append(
                jnp.sum(jnp.where(chosen[:, None, None], terms, 0.0), axis=0)
            )
        slots = jnp.stack(partial_sums).astype(jnp.bfloat16).reshape(members, share, BLOCK)
        sent = pick([slots[s] for s in range(members)], slot_of_member)
        got = lax.all_to_all(sent, "member", 0, 0, tiled=True)
        field = jnp.sum(got.astype(jnp.float32), axis=0)
        residual = (excitations[step, 0] - field).astype(jnp.bfloat16)
        current = jnp.dot(residual, inverses[0], preferred_element_type=jnp.float32)
        results.append(current)
        if step + 1 < STEPS:
            spread = jnp.broadcast_to(current.astype(jnp.bfloat16)[None], (members, share, BLOCK))
            got = lax.all_to_all(spread, "member", 0, 0, tiled=True)
            placed = pick([got[m] for m in range(members)], owners)
            blocks.append(placed.reshape(group_blocks, EXCITE, BLOCK))
    return jnp.stack(results)[:, None]


def solution(mesh):
    placed = (
        P(("group", "member"), None, None),
        P(("group", "member"), None),
        P("group", None),
        P(("group", "member"), None, None),
        P(None, ("group", "member"), None, None),
        P(None, ("group", "member"), None, None),
    )
    return jax.shard_map(
        body,
        mesh=mesh,
        in_specs=placed,
        out_specs=P(None, ("group", "member"), None, None),
        check_vma=False,
    )
```

```python
import jax
import jax.numpy as jnp
from jax import lax
from jax.sharding import PartitionSpec as P

BLOCK = 512
EXCITE = 128
OWNERS = 4
DELAYS = 2
STEPS = 3


def shifted(x, axis, n, k):
    return lax.ppermute(x, axis, [(i, (i + k) % n) for i in range(n)])


def shift_gather(x, axis, n):
    return [x] + [shifted(x, axis, n, k) for k in range(1, n)]


def pick(pieces, index):
    if len(pieces) > 8:
        return jnp.take(jnp.stack(pieces), index, axis=0)
    chosen = index[:, None] == jnp.arange(len(pieces), dtype=index.dtype)[None, :]
    spread = (slice(None),) + (None,) * pieces[0].ndim
    total = None
    for k, piece in enumerate(pieces):
        term = jnp.where(chosen[:, k][spread], piece[None], jnp.zeros_like(piece)[None])
        total = term if total is None else total + term
    return total


def body(tile_values, tile_lists, owner_map, inverses, excitations, history):
    members = lax.axis_size("member")
    groups = lax.axis_size("group")
    group_blocks = members // OWNERS
    share = EXCITE // OWNERS
    group_here = lax.axis_index("group")
    member_here = lax.axis_index("member")
    owners = owner_map[0]
    member_ids = jnp.arange(members, dtype=jnp.int32)
    matches = owners[:, None] == member_ids[None, :]
    slot_of_member = jnp.sum(jnp.where(matches, member_ids[:, None], 0), axis=0)
    send_slot = jnp.take(slot_of_member, (member_here + member_ids) % members)

    spread_hist = jnp.broadcast_to(history[:, 0][None], (members,) + history[:, 0].shape)
    hist_got = lax.all_to_all(spread_hist, "member", 0, 0, tiled=True)
    lists_later, _ = lax.optimization_barrier((tile_lists, spread_hist))
    lists_by_shift = jnp.stack(shift_gather(lists_later, "group", groups))
    group_ids = jnp.arange(groups, dtype=jnp.int32)
    ahead = jnp.take(lists_by_shift, (groups - group_ids) % groups, axis=0)
    wanted = (ahead[:, :, 0] // group_blocks == group_here) & (ahead[:, :, 2] > 0)
    want_block = jnp.sum(jnp.where(wanted, ahead[:, :, 0] % group_blocks, 0), axis=1)
    want_delay = jnp.sum(jnp.where(wanted, ahead[:, :, 2], 0), axis=1)
    block_ids = jnp.arange(group_blocks, dtype=jnp.int32)
    which_block = want_block[:, None] == block_ids[None, :]
    from_near = which_block & (want_delay[:, None] == 1)
    from_far = which_block & (want_delay[:, None] == 2)

    source_group = tile_lists[:, 0] // group_blocks
    observer_local = tile_lists[:, 1] % group_blocks
    delays_here = tile_lists[:, 2]
    source_shift = (group_here - source_group) % groups

    hist_placed = pick([hist_got[m] for m in range(members)], owners)
    blocks = [
        hist_placed[:, t].reshape(group_blocks, EXCITE, BLOCK) for t in range(DELAYS)
    ]
    results = []
    for step in range(STEPS):
        near = blocks[DELAYS + step - 1]
        far = blocks[DELAYS + step - 2]
        outgoing = None
        for block in range(group_blocks):
            term = jnp.where(from_near[:, block, None, None], near[block][None], 0) + jnp.where(
                from_far[:, block, None, None], far[block][None], 0
            )
            outgoing = term if outgoing is None else outgoing + term
        received = [outgoing[0]] + [
            shifted(outgoing[k], "group", groups, k) for k in range(1, groups)
        ]
        blocks_in = pick(received, source_shift)
        terms = jnp.einsum(
            "kes,kso->keo", blocks_in, tile_values, preferred_element_type=jnp.float32
        )
        partial_sums = []
        for block in range(group_blocks):
            chosen = (observer_local == block) & (delays_here > 0)
            partial_sums.append(
                jnp.sum(jnp.where(chosen[:, None, None], terms, 0.0), axis=0)
            )
        slots = jnp.stack(partial_sums).astype(jnp.bfloat16).reshape(members, share, BLOCK)
        sent = pick([slots[s] for s in range(members)], slot_of_member)
        got = lax.all_to_all(sent, "member", 0, 0, tiled=True)
        field = jnp.sum(got.astype(jnp.float32), axis=0)
        residual = (excitations[step, 0] - field).astype(jnp.bfloat16)
        current = jnp.dot(residual, inverses[0], preferred_element_type=jnp.float32)
        results.append(current)
        if step + 1 < STEPS:
            spread = jnp.broadcast_to(current.astype(jnp.bfloat16)[None], (members, share, BLOCK))
            got = lax.all_to_all(spread, "member", 0, 0, tiled=True)
            placed = pick([got[m] for m in range(members)], owners)
            blocks.append(placed.reshape(group_blocks, EXCITE, BLOCK))
    return jnp.stack(results)[:, None]


def solution(mesh):
    placed = (
        P(("group", "member"), None, None),
        P(("group", "member"), None),
        P("group", None),
        P(("group", "member"), None, None),
        P(None, ("group", "member"), None, None),
        P(None, ("group", "member"), None, None),
    )
    return jax.shard_map(
        body,
        mesh=mesh,
        in_specs=placed,
        out_specs=P(None, ("group", "member"), None, None),
        check_vma=False,
    )
```

```python
import jax
import jax.numpy as jnp
from jax import lax
from jax.sharding import PartitionSpec as P

BLOCK = 512
EXCITE = 128
OWNERS = 4
DELAYS = 2
STEPS = 3


def shifted(x, axis, n, k):
    return lax.ppermute(x, axis, [(i, (i + k) % n) for i in range(n)])


def shift_gather(x, axis, n):
    return [x] + [shifted(x, axis, n, k) for k in range(1, n)]


def pick(pieces, index):
    if len(pieces) > 8:
        return jnp.take(jnp.stack(pieces), index, axis=0)
    chosen = index[:, None] == jnp.arange(len(pieces), dtype=index.dtype)[None, :]
    spread = (slice(None),) + (None,) * pieces[0].ndim
    total = None
    for k, piece in enumerate(pieces):
        term = jnp.where(chosen[:, k][spread], piece[None], jnp.zeros_like(piece)[None])
        total = term if total is None else total + term
    return total


def body(tile_values, tile_lists, owner_map, inverses, excitations, history):
    members = lax.axis_size("member")
    groups = lax.axis_size("group")
    group_blocks = members // OWNERS
    share = EXCITE // OWNERS
    group_here = lax.axis_index("group")
    member_here = lax.axis_index("member")
    owners = owner_map[0]
    member_ids = jnp.arange(members, dtype=jnp.int32)
    matches = owners[:, None] == member_ids[None, :]
    slot_of_member = jnp.sum(jnp.where(matches, member_ids[:, None], 0), axis=0)
    send_slot = jnp.take(slot_of_member, (member_here + member_ids) % members)

    spread_hist = jnp.broadcast_to(history[:, 0][None], (members,) + history[:, 0].shape)
    hist_got = lax.all_to_all(spread_hist, "member", 0, 0, tiled=True)
    lists_later, _ = lax.optimization_barrier((tile_lists, spread_hist))
    lists_by_shift = shift_gather(lists_later, "group", groups)
    ahead = jnp.stack([lists_by_shift[(groups - k) % groups] for k in range(groups)])
    wanted = (ahead[:, :, 0] // group_blocks == group_here) & (ahead[:, :, 2] > 0)
    want_block = jnp.sum(jnp.where(wanted, ahead[:, :, 0] % group_blocks, 0), axis=1)
    want_delay = jnp.sum(jnp.where(wanted, ahead[:, :, 2], 0), axis=1)
    block_ids = jnp.arange(group_blocks, dtype=jnp.int32)
    which_block = want_block[:, None] == block_ids[None, :]
    from_near = which_block & (want_delay[:, None] == 1)
    from_far = which_block & (want_delay[:, None] == 2)

    source_group = tile_lists[:, 0] // group_blocks
    observer_local = tile_lists[:, 1] % group_blocks
    delays_here = tile_lists[:, 2]
    source_shift = (group_here - source_group) % groups

    hist_placed = pick([hist_got[m] for m in range(members)], owners)
    blocks = [
        hist_placed[:, t].reshape(group_blocks, EXCITE, BLOCK) for t in range(DELAYS)
    ]
    results = []
    for step in range(STEPS):
        near = blocks[DELAYS + step - 1]
        far = blocks[DELAYS + step - 2]
        outgoing = None
        for block in range(group_blocks):
            term = jnp.where(from_near[:, block, None, None], near[block][None], 0) + jnp.where(
                from_far[:, block, None, None], far[block][None], 0
            )
            outgoing = term if outgoing is None else outgoing + term
        received = [outgoing[0]] + [
            shifted(outgoing[k], "group", groups, k) for k in range(1, groups)
        ]
        blocks_in = pick(received, source_shift)
        terms = jnp.einsum(
            "kes,kso->keo", blocks_in, tile_values, preferred_element_type=jnp.float32
        )
        partial_sums = []
        for block in range(group_blocks):
            chosen = (observer_local == block) & (delays_here > 0)
            partial_sums.append(
                jnp.sum(jnp.where(chosen[:, None, None], terms, 0.0), axis=0)
            )
        slots = jnp.stack(partial_sums).astype(jnp.bfloat16).reshape(members, share, BLOCK)
        sent = pick([slots[s] for s in range(members)], slot_of_member)
        got = lax.all_to_all(sent, "member", 0, 0, tiled=True)
        field = jnp.sum(got.astype(jnp.float32), axis=0)
        residual = (excitations[step, 0] - field).astype(jnp.bfloat16)
        current = jnp.dot(residual, inverses[0], preferred_element_type=jnp.float32)
        results.append(current)
        if step + 1 < STEPS:
            spread = jnp.broadcast_to(current.astype(jnp.bfloat16)[None], (members, share, BLOCK))
            got = lax.all_to_all(spread, "member", 0, 0, tiled=True)
            placed = pick([got[m] for m in range(members)], owners)
            blocks.append(placed.reshape(group_blocks, EXCITE, BLOCK))
    return jnp.stack(results)[:, None]


def solution(mesh):
    placed = (
        P(("group", "member"), None, None),
        P(("group", "member"), None),
        P("group", None),
        P(("group", "member"), None, None),
        P(None, ("group", "member"), None, None),
        P(None, ("group", "member"), None, None),
    )
    return jax.shard_map(
        body,
        mesh=mesh,
        in_specs=placed,
        out_specs=P(None, ("group", "member"), None, None),
        check_vma=False,
    )
```

```python
import jax
import jax.numpy as jnp
from jax import lax
from jax.sharding import PartitionSpec as P

BLOCK = 512
EXCITE = 128
OWNERS = 4
DELAYS = 2
STEPS = 3


def shifted(x, axis, n, k):
    return lax.ppermute(x, axis, [(i, (i + k) % n) for i in range(n)])


def shift_gather(x, axis, n):
    return [x] + [shifted(x, axis, n, k) for k in range(1, n)]


def pick(pieces, index):
    if len(pieces) > 8:
        return jnp.take(jnp.stack(pieces), index, axis=0)
    chosen = index[:, None] == jnp.arange(len(pieces), dtype=index.dtype)[None, :]
    spread = (slice(None),) + (None,) * pieces[0].ndim
    total = None
    for k, piece in enumerate(pieces):
        term = jnp.where(chosen[:, k][spread], piece[None], jnp.zeros_like(piece)[None])
        total = term if total is None else total + term
    return total


def body(tile_values, tile_lists, owner_map, inverses, excitations, history):
    members = lax.axis_size("member")
    groups = lax.axis_size("group")
    group_blocks = members // OWNERS
    share = EXCITE // OWNERS
    group_here = lax.axis_index("group")
    member_here = lax.axis_index("member")
    owners = owner_map[0]
    member_ids = jnp.arange(members, dtype=jnp.int32)

    spread_hist = jnp.broadcast_to(history[:, 0][None], (members,) + history[:, 0].shape)
    hist_got = lax.all_to_all(spread_hist, "member", 0, 0, tiled=True)
    lists_later, _ = lax.optimization_barrier((tile_lists, spread_hist))
    lists_by_shift = shift_gather(lists_later, "group", groups)
    ahead = jnp.stack([lists_by_shift[(groups - k) % groups] for k in range(groups)])
    wanted = (ahead[:, :, 0] // group_blocks == group_here) & (ahead[:, :, 2] > 0)
    want_block = jnp.sum(jnp.where(wanted, ahead[:, :, 0] % group_blocks, 0), axis=1)
    want_delay = jnp.sum(jnp.where(wanted, ahead[:, :, 2], 0), axis=1)
    block_ids = jnp.arange(group_blocks, dtype=jnp.int32)
    which_block = want_block[:, None] == block_ids[None, :]
    from_near = which_block & (want_delay[:, None] == 1)
    from_far = which_block & (want_delay[:, None] == 2)

    hist_placed = pick([hist_got[m] for m in range(members)], owners)
    blocks = [
        hist_placed[:, t].reshape(group_blocks, EXCITE, BLOCK) for t in range(DELAYS)
    ]
    results = []
    for step in range(STEPS):
        near = blocks[DELAYS + step - 1]
        far = blocks[DELAYS + step - 2]
        outgoing = None
        for block in range(group_blocks):
            term = jnp.where(from_near[:, block, None, None], near[block][None], 0) + jnp.where(
                from_far[:, block, None, None], far[block][None], 0
            )
            outgoing = term if outgoing is None else outgoing + term
        received = [outgoing[0]] + [
            shifted(outgoing[k], "group", groups, k) for k in range(1, groups)
        ]
        if step == 0:
            late_lists, late_owners, _ = lax.optimization_barrier(
                (tile_lists, owners, received[groups - 1])
            )
            matches = late_owners[:, None] == member_ids[None, :]
            slot_of_member = jnp.sum(jnp.where(matches, member_ids[:, None], 0), axis=0)
            observer_local = late_lists[:, 1] % group_blocks
            delays_here = late_lists[:, 2]
            source_shift = (group_here - late_lists[:, 0] // group_blocks) % groups
        blocks_in = pick(received, source_shift)
        terms = jnp.einsum(
            "kes,kso->keo", blocks_in, tile_values, preferred_element_type=jnp.float32
        )
        partial_sums = []
        for block in range(group_blocks):
            chosen = (observer_local == block) & (delays_here > 0)
            partial_sums.append(
                jnp.sum(jnp.where(chosen[:, None, None], terms, 0.0), axis=0)
            )
        slots = jnp.stack(partial_sums).astype(jnp.bfloat16).reshape(members, share, BLOCK)
        sent = pick([slots[s] for s in range(members)], slot_of_member)
        got = lax.all_to_all(sent, "member", 0, 0, tiled=True)
        field = jnp.sum(got.astype(jnp.float32), axis=0)
        residual = (excitations[step, 0] - field).astype(jnp.bfloat16)
        current = jnp.dot(residual, inverses[0], preferred_element_type=jnp.float32)
        results.append(current)
        if step + 1 < STEPS:
            spread = jnp.broadcast_to(current.astype(jnp.bfloat16)[None], (members, share, BLOCK))
            got = lax.all_to_all(spread, "member", 0, 0, tiled=True)
            placed = pick([got[m] for m in range(members)], owners)
            blocks.append(placed.reshape(group_blocks, EXCITE, BLOCK))
    return jnp.stack(results)[:, None]


def solution(mesh):
    placed = (
        P(("group", "member"), None, None),
        P(("group", "member"), None),
        P("group", None),
        P(("group", "member"), None, None),
        P(None, ("group", "member"), None, None),
        P(None, ("group", "member"), None, None),
    )
    return jax.shard_map(
        body,
        mesh=mesh,
        in_specs=placed,
        out_specs=P(None, ("group", "member"), None, None),
        check_vma=False,
    )
```

```python
import jax
import jax.numpy as jnp
from jax import lax
from jax.sharding import PartitionSpec as P

BLOCK = 512
EXCITE = 128
OWNERS = 4
DELAYS = 2
STEPS = 3


def shifted(x, axis, n, k):
    return lax.ppermute(x, axis, [(i, (i + k) % n) for i in range(n)])


def shift_gather(x, axis, n):
    return [x] + [shifted(x, axis, n, k) for k in range(1, n)]


def pick(pieces, index):
    if len(pieces) > 8:
        return jnp.take(jnp.stack(pieces), index, axis=0)
    chosen = index[:, None] == jnp.arange(len(pieces), dtype=index.dtype)[None, :]
    spread = (slice(None),) + (None,) * pieces[0].ndim
    total = None
    for k, piece in enumerate(pieces):
        term = jnp.where(chosen[:, k][spread], piece[None], jnp.zeros_like(piece)[None])
        total = term if total is None else total + term
    return total


def body(tile_values, tile_lists, owner_map, inverses, excitations, history):
    members = lax.axis_size("member")
    groups = lax.axis_size("group")
    group_blocks = members // OWNERS
    share = EXCITE // OWNERS
    group_here = lax.axis_index("group")
    member_here = lax.axis_index("member")
    owners = owner_map[0]
    member_ids = jnp.arange(members, dtype=jnp.int32)

    spread_hist = jnp.broadcast_to(history[:, 0][None], (members,) + history[:, 0].shape)
    hist_got = lax.all_to_all(spread_hist, "member", 0, 0, tiled=True)
    lists_later, _ = lax.optimization_barrier((tile_lists, spread_hist))
    lists_by_group = lax.all_gather(lists_later, "group", axis=0, tiled=False)
    ahead = jnp.take(lists_by_group, (group_here + jnp.arange(groups)) % groups, axis=0)
    wanted = (ahead[:, :, 0] // group_blocks == group_here) & (ahead[:, :, 2] > 0)
    want_block = jnp.sum(jnp.where(wanted, ahead[:, :, 0] % group_blocks, 0), axis=1)
    want_delay = jnp.sum(jnp.where(wanted, ahead[:, :, 2], 0), axis=1)
    block_ids = jnp.arange(group_blocks, dtype=jnp.int32)
    which_block = want_block[:, None] == block_ids[None, :]
    from_near = which_block & (want_delay[:, None] == 1)
    from_far = which_block & (want_delay[:, None] == 2)

    hist_placed = pick([hist_got[m] for m in range(members)], owners)
    blocks = [
        hist_placed[:, t].reshape(group_blocks, EXCITE, BLOCK) for t in range(DELAYS)
    ]
    results = []
    for step in range(STEPS):
        near = blocks[DELAYS + step - 1]
        far = blocks[DELAYS + step - 2]
        outgoing = None
        for block in range(group_blocks):
            term = jnp.where(from_near[:, block, None, None], near[block][None], 0) + jnp.where(
                from_far[:, block, None, None], far[block][None], 0
            )
            outgoing = term if outgoing is None else outgoing + term
        received = [outgoing[0]] + [
            shifted(outgoing[k], "group", groups, k) for k in range(1, groups)
        ]
        if step == 0:
            late_lists, late_owners, _ = lax.optimization_barrier(
                (tile_lists, owners, received[groups - 1])
            )
            matches = late_owners[:, None] == member_ids[None, :]
            slot_of_member = jnp.sum(jnp.where(matches, member_ids[:, None], 0), axis=0)
            observer_local = late_lists[:, 1] % group_blocks
            delays_here = late_lists[:, 2]
            source_shift = (group_here - late_lists[:, 0] // group_blocks) % groups
        blocks_in = pick(received, source_shift)
        terms = jnp.einsum(
            "kes,kso->keo", blocks_in, tile_values, preferred_element_type=jnp.float32
        )
        partial_sums = []
        for block in range(group_blocks):
            chosen = (observer_local == block) & (delays_here > 0)
            partial_sums.append(
                jnp.sum(jnp.where(chosen[:, None, None], terms, 0.0), axis=0)
            )
        slots = jnp.stack(partial_sums).astype(jnp.bfloat16).reshape(members, share, BLOCK)
        sent = pick([slots[s] for s in range(members)], slot_of_member)
        got = lax.all_to_all(sent, "member", 0, 0, tiled=True)
        field = jnp.sum(got.astype(jnp.float32), axis=0)
        residual = (excitations[step, 0] - field).astype(jnp.bfloat16)
        current = jnp.dot(residual, inverses[0], preferred_element_type=jnp.float32)
        results.append(current)
        if step + 1 < STEPS:
            spread = jnp.broadcast_to(current.astype(jnp.bfloat16)[None], (members, share, BLOCK))
            got = lax.all_to_all(spread, "member", 0, 0, tiled=True)
            placed = pick([got[m] for m in range(members)], owners)
            blocks.append(placed.reshape(group_blocks, EXCITE, BLOCK))
    return jnp.stack(results)[:, None]


def solution(mesh):
    placed = (
        P(("group", "member"), None, None),
        P(("group", "member"), None),
        P("group", None),
        P(("group", "member"), None, None),
        P(None, ("group", "member"), None, None),
        P(None, ("group", "member"), None, None),
    )
    return jax.shard_map(
        body,
        mesh=mesh,
        in_specs=placed,
        out_specs=P(None, ("group", "member"), None, None),
        check_vma=False,
    )
```

```python
import jax
import jax.numpy as jnp
from jax import lax
from jax.sharding import PartitionSpec as P

BLOCK = 512
EXCITE = 128
OWNERS = 4
DELAYS = 2
STEPS = 3


def shifted(x, axis, n, k):
    return lax.ppermute(x, axis, [(i, (i + k) % n) for i in range(n)])


def shift_gather(x, axis, n):
    return [x] + [shifted(x, axis, n, k) for k in range(1, n)]


def pick(pieces, index):
    if len(pieces) > 8:
        return jnp.take(jnp.stack(pieces), index, axis=0)
    chosen = index[:, None] == jnp.arange(len(pieces), dtype=index.dtype)[None, :]
    spread = (slice(None),) + (None,) * pieces[0].ndim
    total = None
    for k, piece in enumerate(pieces):
        term = jnp.where(chosen[:, k][spread], piece[None], jnp.zeros_like(piece)[None])
        total = term if total is None else total + term
    return total


def body(tile_values, tile_lists, owner_map, inverses, excitations, history):
    members = lax.axis_size("member")
    groups = lax.axis_size("group")
    group_blocks = members // OWNERS
    share = EXCITE // OWNERS
    group_here = lax.axis_index("group")
    member_here = lax.axis_index("member")
    owners = owner_map[0]
    member_ids = jnp.arange(members, dtype=jnp.int32)

    spread_hist = jnp.broadcast_to(history[:, 0][None], (members,) + history[:, 0].shape)
    hist_got = lax.all_to_all(spread_hist, "member", 0, 0, tiled=True)
    lists_later, _ = lax.optimization_barrier((tile_lists, spread_hist))
    lists_by_shift = shift_gather(lists_later, "group", groups)
    ahead = jnp.stack([lists_by_shift[(groups - k) % groups] for k in range(groups)])
    wanted = (ahead[:, :, 0] // group_blocks == group_here) & (ahead[:, :, 2] > 0)
    want_block = jnp.sum(jnp.where(wanted, ahead[:, :, 0] % group_blocks, 0), axis=1)
    want_delay = jnp.sum(jnp.where(wanted, ahead[:, :, 2], 0), axis=1)
    block_ids = jnp.arange(group_blocks, dtype=jnp.int32)
    which_block = want_block[:, None] == block_ids[None, :]
    from_near = which_block & (want_delay[:, None] == 1)
    from_far = which_block & (want_delay[:, None] == 2)

    hist_placed = pick([hist_got[m] for m in range(members)], owners)
    blocks = [
        hist_placed[:, t].reshape(group_blocks, EXCITE, BLOCK) for t in range(DELAYS)
    ]
    results = []
    for step in range(STEPS):
        near = blocks[DELAYS + step - 1]
        far = blocks[DELAYS + step - 2]
        outgoing = None
        for block in range(group_blocks):
            term = jnp.where(from_near[:, block, None, None], near[block][None], 0) + jnp.where(
                from_far[:, block, None, None], far[block][None], 0
            )
            outgoing = term if outgoing is None else outgoing + term
        received = [outgoing[0]] + [
            shifted(outgoing[k], "group", groups, k) for k in range(1, groups)
        ]
        if step == 0:
            late_lists, late_owners, _ = lax.optimization_barrier(
                (tile_lists, owners, received[groups - 1])
            )
            matches = late_owners[:, None] == member_ids[None, :]
            slot_of_member = jnp.sum(jnp.where(matches, member_ids[:, None], 0), axis=0)
            observer_local = late_lists[:, 1] % group_blocks
            delays_here = late_lists[:, 2]
            source_shift = (group_here - late_lists[:, 0] // group_blocks) % groups
        blocks_in = pick(received, source_shift)
        terms = jnp.einsum(
            "kes,kso->keo", blocks_in, tile_values, preferred_element_type=jnp.float32
        )
        partial_sums = []
        for block in range(group_blocks):
            chosen = (observer_local == block) & (delays_here > 0)
            partial_sums.append(
                jnp.sum(jnp.where(chosen[:, None, None], terms, 0.0), axis=0)
            )
        slots = jnp.stack(partial_sums).astype(jnp.bfloat16).reshape(members, share, BLOCK)
        sent = pick([slots[s] for s in range(members)], slot_of_member)
        got = lax.all_to_all(sent, "member", 0, 0, tiled=True)
        field = jnp.sum(got.astype(jnp.float32), axis=0)
        residual = (excitations[step, 0] - field).astype(jnp.bfloat16)
        current = jnp.dot(residual, inverses[0], preferred_element_type=jnp.float32)
        results.append(current)
        if step + 1 < STEPS:
            got = lax.all_gather(current.astype(jnp.bfloat16), "member", axis=0, tiled=False)
            placed = pick([got[m] for m in range(members)], owners)
            blocks.append(placed.reshape(group_blocks, EXCITE, BLOCK))
    return jnp.stack(results)[:, None]


def solution(mesh):
    placed = (
        P(("group", "member"), None, None),
        P(("group", "member"), None),
        P("group", None),
        P(("group", "member"), None, None),
        P(None, ("group", "member"), None, None),
        P(None, ("group", "member"), None, None),
    )
    return jax.shard_map(
        body,
        mesh=mesh,
        in_specs=placed,
        out_specs=P(None, ("group", "member"), None, None),
        check_vma=False,
    )
```

```python
import jax
import jax.numpy as jnp
from jax import lax
from jax.sharding import PartitionSpec as P

BLOCK = 512
EXCITE = 128
OWNERS = 4
DELAYS = 2
STEPS = 3


def shifted(x, axis, n, k):
    return lax.ppermute(x, axis, [(i, (i + k) % n) for i in range(n)])


def shift_gather(x, axis, n):
    return [x] + [shifted(x, axis, n, k) for k in range(1, n)]


def pick(pieces, index):
    if len(pieces) > 8:
        return jnp.take(jnp.stack(pieces), index, axis=0)
    chosen = index[:, None] == jnp.arange(len(pieces), dtype=index.dtype)[None, :]
    spread = (slice(None),) + (None,) * pieces[0].ndim
    total = None
    for k, piece in enumerate(pieces):
        term = jnp.where(chosen[:, k][spread], piece[None], jnp.zeros_like(piece)[None])
        total = term if total is None else total + term
    return total


def body(tile_values, tile_lists, owner_map, inverses, excitations, history):
    members = lax.axis_size("member")
    groups = lax.axis_size("group")
    group_blocks = members // OWNERS
    share = EXCITE // OWNERS
    group_here = lax.axis_index("group")
    member_here = lax.axis_index("member")
    owners = owner_map[0]
    member_ids = jnp.arange(members, dtype=jnp.int32)

    spread_hist = jnp.broadcast_to(history[:, 0][None], (members,) + history[:, 0].shape)
    hist_got = lax.all_to_all(spread_hist, "member", 0, 0, tiled=True)
    lists_later, _ = lax.optimization_barrier((tile_lists, spread_hist))
    lists_by_shift = shift_gather(lists_later, "group", groups)
    ahead = jnp.stack([lists_by_shift[(groups - k) % groups] for k in range(groups)])
    wanted = (ahead[:, :, 0] // group_blocks == group_here) & (ahead[:, :, 2] > 0)
    want_block = jnp.sum(jnp.where(wanted, ahead[:, :, 0] % group_blocks, 0), axis=1)
    want_delay = jnp.sum(jnp.where(wanted, ahead[:, :, 2], 0), axis=1)
    owner_of_row = owners[OWNERS * want_block[:, None] + jnp.arange(OWNERS, dtype=jnp.int32)[None, :]]
    row_from = owner_of_row[:, :, None] == member_ids[None, None, :]
    from_near = row_from & (want_delay[:, None, None] == 1)
    from_far = row_from & (want_delay[:, None, None] == 2)

    times = [hist_got[:, t] for t in range(DELAYS)]
    results = []
    for step in range(STEPS):
        near = times[DELAYS + step - 1]
        far = times[DELAYS + step - 2]
        outgoing = None
        for m in range(members):
            term = jnp.where(from_near[:, :, m, None, None], near[m][None, None], 0) + jnp.where(
                from_far[:, :, m, None, None], far[m][None, None], 0
            )
            outgoing = term if outgoing is None else outgoing + term
        outgoing = outgoing.reshape(groups, EXCITE, BLOCK)
        received = [outgoing[0]] + [
            shifted(outgoing[k], "group", groups, k) for k in range(1, groups)
        ]
        if step == 0:
            late_lists, late_owners, _ = lax.optimization_barrier(
                (tile_lists, owners, received[groups - 1])
            )
            matches = late_owners[:, None] == member_ids[None, :]
            slot_of_member = jnp.sum(jnp.where(matches, member_ids[:, None], 0), axis=0)
            observer_local = late_lists[:, 1] % group_blocks
            delays_here = late_lists[:, 2]
            source_shift = (group_here - late_lists[:, 0] // group_blocks) % groups
        blocks_in = pick(received, source_shift)
        terms = jnp.einsum(
            "kes,kso->keo", blocks_in, tile_values, preferred_element_type=jnp.float32
        )
        partial_sums = []
        for block in range(group_blocks):
            chosen = (observer_local == block) & (delays_here > 0)
            partial_sums.append(
                jnp.sum(jnp.where(chosen[:, None, None], terms, 0.0), axis=0)
            )
        slots = jnp.stack(partial_sums).astype(jnp.bfloat16).reshape(members, share, BLOCK)
        sent = pick([slots[s] for s in range(members)], slot_of_member)
        got = lax.all_to_all(sent, "member", 0, 0, tiled=True)
        field = jnp.sum(got.astype(jnp.float32), axis=0)
        residual = (excitations[step, 0] - field).astype(jnp.bfloat16)
        current = jnp.dot(residual, inverses[0], preferred_element_type=jnp.float32)
        results.append(current)
        if step + 1 < STEPS:
            spread = jnp.broadcast_to(current.astype(jnp.bfloat16)[None], (members, share, BLOCK))
            times.append(lax.all_to_all(spread, "member", 0, 0, tiled=True))
    return jnp.stack(results)[:, None]


def solution(mesh):
    placed = (
        P(("group", "member"), None, None),
        P(("group", "member"), None),
        P("group", None),
        P(("group", "member"), None, None),
        P(None, ("group", "member"), None, None),
        P(None, ("group", "member"), None, None),
    )
    return jax.shard_map(
        body,
        mesh=mesh,
        in_specs=placed,
        out_specs=P(None, ("group", "member"), None, None),
        check_vma=False,
    )
```

```python
import jax
import jax.numpy as jnp
from jax import lax
from jax.sharding import PartitionSpec as P

BLOCK = 512
EXCITE = 128
OWNERS = 4
DELAYS = 2
STEPS = 3


def shifted(x, axis, n, k):
    return lax.ppermute(x, axis, [(i, (i + k) % n) for i in range(n)])


def shift_gather(x, axis, n):
    return [x] + [shifted(x, axis, n, k) for k in range(1, n)]


def pick(pieces, index):
    if len(pieces) > 8:
        return jnp.take(jnp.stack(pieces), index, axis=0)
    chosen = index[:, None] == jnp.arange(len(pieces), dtype=index.dtype)[None, :]
    spread = (slice(None),) + (None,) * pieces[0].ndim
    total = None
    for k, piece in enumerate(pieces):
        term = jnp.where(chosen[:, k][spread], piece[None], jnp.zeros_like(piece)[None])
        total = term if total is None else total + term
    return total


def body(tile_values, tile_lists, owner_map, inverses, excitations, history):
    members = lax.axis_size("member")
    groups = lax.axis_size("group")
    group_blocks = members // OWNERS
    share = EXCITE // OWNERS
    group_here = lax.axis_index("group")
    member_here = lax.axis_index("member")
    owners = owner_map[0]
    member_ids = jnp.arange(members, dtype=jnp.int32)

    spread_hist = jnp.broadcast_to(history[:, 0][None], (members,) + history[:, 0].shape)
    hist_got = lax.all_to_all(spread_hist, "member", 0, 0, tiled=True)
    lists_later, _ = lax.optimization_barrier((tile_lists, spread_hist))
    lists_by_shift = shift_gather(lists_later, "group", groups)
    ahead = jnp.stack([lists_by_shift[(groups - k) % groups] for k in range(groups)])
    wanted = (ahead[:, :, 0] // group_blocks == group_here) & (ahead[:, :, 2] > 0)
    want_block = jnp.sum(jnp.where(wanted, ahead[:, :, 0] % group_blocks, 0), axis=1)
    want_delay = jnp.sum(jnp.where(wanted, ahead[:, :, 2], 0), axis=1)
    block_ids = jnp.arange(group_blocks, dtype=jnp.int32)
    which_block = want_block[:, None] == block_ids[None, :]
    from_near = which_block & (want_delay[:, None] == 1)
    from_far = which_block & (want_delay[:, None] == 2)

    hist_placed = pick([hist_got[m] for m in range(members)], owners)
    blocks = [
        hist_placed[:, t].reshape(group_blocks, EXCITE, BLOCK) for t in range(DELAYS)
    ]
    results = jnp.zeros((STEPS, 1, share, BLOCK), jnp.float32)
    for step in range(STEPS):
        near = blocks[DELAYS + step - 1]
        far = blocks[DELAYS + step - 2]
        outgoing = None
        for block in range(group_blocks):
            term = jnp.where(from_near[:, block, None, None], near[block][None], 0) + jnp.where(
                from_far[:, block, None, None], far[block][None], 0
            )
            outgoing = term if outgoing is None else outgoing + term
        received = [outgoing[0]] + [
            shifted(outgoing[k], "group", groups, k) for k in range(1, groups)
        ]
        if step == 0:
            late_lists, late_owners, _ = lax.optimization_barrier(
                (tile_lists, owners, received[groups - 1])
            )
            matches = late_owners[:, None] == member_ids[None, :]
            slot_of_member = jnp.sum(jnp.where(matches, member_ids[:, None], 0), axis=0)
            observer_local = late_lists[:, 1] % group_blocks
            delays_here = late_lists[:, 2]
            source_shift = (group_here - late_lists[:, 0] // group_blocks) % groups
        blocks_in = pick(received, source_shift)
        terms = jnp.einsum(
            "kes,kso->keo", blocks_in, tile_values, preferred_element_type=jnp.float32
        )
        partial_sums = []
        for block in range(group_blocks):
            chosen = (observer_local == block) & (delays_here > 0)
            partial_sums.append(
                jnp.sum(jnp.where(chosen[:, None, None], terms, 0.0), axis=0)
            )
        slots = jnp.stack(partial_sums).astype(jnp.bfloat16).reshape(members, share, BLOCK)
        sent = pick([slots[s] for s in range(members)], slot_of_member)
        got = lax.all_to_all(sent, "member", 0, 0, tiled=True)
        field = jnp.sum(got.astype(jnp.float32), axis=0)
        residual = (excitations[step, 0] - field).astype(jnp.bfloat16)
        current = jnp.dot(residual, inverses[0], preferred_element_type=jnp.float32)
        results = lax.dynamic_update_slice(results, current[None, None], (step, 0, 0, 0))
        if step + 1 < STEPS:
            spread = jnp.broadcast_to(current.astype(jnp.bfloat16)[None], (members, share, BLOCK))
            got = lax.all_to_all(spread, "member", 0, 0, tiled=True)
            placed = pick([got[m] for m in range(members)], owners)
            blocks.append(placed.reshape(group_blocks, EXCITE, BLOCK))
    return results


def solution(mesh):
    placed = (
        P(("group", "member"), None, None),
        P(("group", "member"), None),
        P("group", None),
        P(("group", "member"), None, None),
        P(None, ("group", "member"), None, None),
        P(None, ("group", "member"), None, None),
    )
    return jax.shard_map(
        body,
        mesh=mesh,
        in_specs=placed,
        out_specs=P(None, ("group", "member"), None, None),
        check_vma=False,
    )
```

```python
import jax
import jax.numpy as jnp
from jax import lax
from jax.sharding import PartitionSpec as P

BLOCK = 512
EXCITE = 128
OWNERS = 4
DELAYS = 2
STEPS = 3


def shifted(x, axis, n, k):
    return lax.ppermute(x, axis, [(i, (i + k) % n) for i in range(n)])


def shift_gather(x, axis, n):
    return [x] + [shifted(x, axis, n, k) for k in range(1, n)]


def pick(pieces, index):
    if len(pieces) > 8:
        return jnp.take(jnp.stack(pieces), index, axis=0)
    chosen = index[:, None] == jnp.arange(len(pieces), dtype=index.dtype)[None, :]
    spread = (slice(None),) + (None,) * pieces[0].ndim
    total = None
    for k, piece in enumerate(pieces):
        term = jnp.where(chosen[:, k][spread], piece[None], jnp.zeros_like(piece)[None])
        total = term if total is None else total + term
    return total


def body(tile_values, tile_lists, owner_map, inverses, excitations, history):
    members = lax.axis_size("member")
    groups = lax.axis_size("group")
    group_blocks = members // OWNERS
    share = EXCITE // OWNERS
    group_here = lax.axis_index("group")
    member_here = lax.axis_index("member")
    owners = owner_map[0]
    member_ids = jnp.arange(members, dtype=jnp.int32)

    spread_hist = jnp.broadcast_to(history[:, 0][None], (members,) + history[:, 0].shape)
    hist_got = lax.all_to_all(spread_hist, "member", 0, 0, tiled=True)
    lists_later, _ = lax.optimization_barrier((tile_lists, spread_hist))
    lists_by_shift = shift_gather(lists_later, "group", groups)
    ahead = jnp.stack([lists_by_shift[(groups - k) % groups] for k in range(groups)])
    wanted = (ahead[:, :, 0] // group_blocks == group_here) & (ahead[:, :, 2] > 0)
    want_block = jnp.sum(jnp.where(wanted, ahead[:, :, 0] % group_blocks, 0), axis=1)
    want_delay = jnp.sum(jnp.where(wanted, ahead[:, :, 2], 0), axis=1)
    block_ids = jnp.arange(group_blocks, dtype=jnp.int32)
    which_block = want_block[:, None] == block_ids[None, :]
    from_near = which_block & (want_delay[:, None] == 1)
    from_far = which_block & (want_delay[:, None] == 2)

    hist_placed = pick([hist_got[m] for m in range(members)], owners)
    blocks = [
        hist_placed[:, t].reshape(group_blocks, EXCITE, BLOCK) for t in range(DELAYS)
    ]
    results = []
    for step in range(STEPS):
        near = blocks[DELAYS + step - 1]
        far = blocks[DELAYS + step - 2]
        outgoing = None
        for block in range(group_blocks):
            term = jnp.where(from_near[:, block, None, None], near[block][None], 0) + jnp.where(
                from_far[:, block, None, None], far[block][None], 0
            )
            outgoing = term if outgoing is None else outgoing + term
        received = [outgoing[0]] + [
            shifted(outgoing[k], "group", groups, k) for k in range(1, groups)
        ]
        if step == 0:
            late_lists, late_owners, _ = lax.optimization_barrier(
                (tile_lists, owners, received[groups - 1])
            )
            matches = late_owners[:, None] == member_ids[None, :]
            slot_of_member = jnp.sum(jnp.where(matches, member_ids[:, None], 0), axis=0)
            observer_local = late_lists[:, 1] % group_blocks
            delays_here = late_lists[:, 2]
            source_shift = (group_here - late_lists[:, 0] // group_blocks) % groups
            live_here = (delays_here > 0)[None, :, None]
            same_block = observer_local[None, :, None] == (slot_of_member // OWNERS)[:, None, None]
            same_share = jnp.arange(OWNERS)[None, None, :] == (slot_of_member % OWNERS)[:, None, None]
            to_member = live_here & same_block & same_share
        blocks_in = pick(received, source_shift)
        terms = jnp.einsum(
            "kes,kso->keo", blocks_in, tile_values, preferred_element_type=jnp.float32
        )
        by_share = terms.reshape(terms.shape[0], OWNERS, share, BLOCK)
        sent = None
        for i in range(terms.shape[0]):
            for q in range(OWNERS):
                chosen = to_member[:, i, q, None, None]
                term = jnp.where(chosen, by_share[i, q][None], 0.0)
                sent = term if sent is None else sent + term
        sent = sent.astype(jnp.bfloat16)
        got = lax.all_to_all(sent, "member", 0, 0, tiled=True)
        field = jnp.sum(got.astype(jnp.float32), axis=0)
        residual = (excitations[step, 0] - field).astype(jnp.bfloat16)
        current = jnp.dot(residual, inverses[0], preferred_element_type=jnp.float32)
        results.append(current)
        if step + 1 < STEPS:
            spread = jnp.broadcast_to(current.astype(jnp.bfloat16)[None], (members, share, BLOCK))
            got = lax.all_to_all(spread, "member", 0, 0, tiled=True)
            placed = pick([got[m] for m in range(members)], owners)
            blocks.append(placed.reshape(group_blocks, EXCITE, BLOCK))
    return jnp.stack(results)[:, None]


def solution(mesh):
    placed = (
        P(("group", "member"), None, None),
        P(("group", "member"), None),
        P("group", None),
        P(("group", "member"), None, None),
        P(None, ("group", "member"), None, None),
        P(None, ("group", "member"), None, None),
    )
    return jax.shard_map(
        body,
        mesh=mesh,
        in_specs=placed,
        out_specs=P(None, ("group", "member"), None, None),
        check_vma=False,
    )
```
